128 devices in a mesh: shot: 32 (over z, x, core), az: 4 (over y).
Axes of the slice: x: 4, y: 4, z: 4, core: 2. Of those that a mesh axis runs over, the one named last changes fastest.
Arguments:
- spectra: bfloat16 [4, 128, 4096, 128], P('az', None, 'shot'), may hold values from -6 to 6
- sampled_mask: int32 [4, 128, 16, 256], P('az', 'shot'), may hold values 0 or 1
- counts: int32 [4, 128], P('az', 'shot'), may hold values from 1 to 6, as said below
Outputs:
- blended: bfloat16 [4, 128, 2048, 128], P('az', None, 'shot')
The draws below stay inside these ranges and needn't reach their ends.
Inputs may be any that keep to these rules, and one draw needn't show every extreme that they name: `counts`: every draw holds a patch with 1 iteration and a patch with 6.
All inputs are finite; a program needn't handle non-finite values. No bound on the sum of `sampled_mask` on one device may be relied on, other than what follows from the above.
Results may differ from the reference program's by a relative error of at most 0.008.
Values may be sent and summed in bfloat16 or wider, within the bound.
No kernel may reach another device: no remote copies, remote signals or barrier semaphores. Data moves between devices by JAX's collectives and lax.ppermute only.
A program may use at most 64 MiB of HBM per device.

```python
import jax
import jax.numpy as jnp
from jax import lax

SIDE = 16
FREQ = 64
MAXIT = 6
PATCH_DEV = 4
NAZ = 4
P_AZ = 128


def draw_counts(key, part):
    light = jax.random.randint(key, (NAZ * P_AZ,), 0, 2, dtype=jnp.int32)
    heavy = jax.random.randint(jax.random.fold_in(key, 3), (NAZ * P_AZ,), 2, MAXIT + 1, dtype=jnp.int32)
    base = jnp.where(light == 0, jnp.ones_like(heavy), heavy).reshape(NAZ, P_AZ)
    base = base.at[0, :PATCH_DEV].set(MAXIT).at[1, :PATCH_DEV].set(1)
    return base


def plant(entries, own_key, smallest, top_value):
    shape = entries.shape
    index_at = [jax.random.randint(jax.random.fold_in(own_key, axis), (), 0, shape[axis]) for axis in range(len(shape))]
    entries = entries.at[tuple(index_at)].set(smallest)
    longest = shape.index(max(shape))
    index_at[longest] = (index_at[longest] + 1) % shape[longest]
    return entries.at[tuple(index_at)].set(top_value)


def shard_levels(own_key, shape, split, low, high):
    def one(dim, parts):
        draws = jax.random.uniform(jax.random.fold_in(jax.random.fold_in(own_key, 6), dim), (parts,), jnp.float32, low / len(split), high / len(split))
        return jnp.repeat(jnp.exp(draws), shape[dim] // parts).reshape((-1,) + (1,) * (len(shape) - dim - 1))

    factor_of = one(*split[0])
    for cut in split[1:]:
        factor_of = factor_of * one(*cut)
    return factor_of


def normal_values(stream_key, shape, scale, reach, shards=(), kind=jnp.bfloat16):
    values = jax.random.normal(stream_key, shape, jnp.float32) * scale
    if len(shards) > 0:
        values = shard_levels(stream_key, shape, shards, -0.22, 0.18) * values
    return jnp.clip(values, min=-reach, max=reach).astype(kind)


def setup_inputs(seed: int = 0) -> dict:
    seeds = jax.random.split(jax.random.key(seed), 4)
    spectra = normal_values(seeds[0], (NAZ, P_AZ, SIDE**3, 2 * FREQ), 1.0, 6.0, ((0, 4), (2, 32)))
    sampled_mask = plant((jax.random.randint(seeds[1], (NAZ, P_AZ, SIDE, SIDE * SIDE), 0, 2) < 1).astype(jnp.int32), jax.random.fold_in(seeds[1], 1), 0, 1)
    counts = draw_counts(jax.random.fold_in(seeds[3], 71), 0)
    return {"spectra": spectra, "sampled_mask": sampled_mask, "counts": counts}


def dft_tables(extent):
    indices = jnp.arange(extent, dtype=jnp.int32)
    product = indices[:, None] * indices[None, :] % extent
    phase = product.astype(jnp.float32) * (2.0 * jnp.pi / extent)
    scale = extent ** (-0.5)
    cos_table = jnp.cos(phase) * scale
    sin_table = -jnp.sin(phase) * scale
    kron_real = jnp.kron(cos_table, cos_table) - jnp.kron(sin_table, sin_table)
    kron_imag = jnp.kron(cos_table, sin_table) + jnp.kron(sin_table, cos_table)
    return (cos_table.astype(jnp.bfloat16), sin_table.astype(jnp.bfloat16), kron_real.astype(jnp.bfloat16), kron_imag.astype(jnp.bfloat16))

def apply_along(mat_real, mat_imag, volume, pattern):
    halfway = volume.shape[-1] // 2
    rotated = jnp.concatenate([-volume[..., halfway:], volume[..., :halfway]], axis=-1)
    first_part = jnp.einsum(pattern, mat_real.astype(jnp.float32), volume.astype(jnp.float32), precision=lax.Precision.HIGHEST)
    second_part = jnp.einsum(pattern, mat_imag.astype(jnp.float32), rotated.astype(jnp.float32), precision=lax.Precision.HIGHEST)
    return first_part + second_part

def project_patch(observed, mask_item, sweeps, tables):
    cos_table, sin_table, kron_real, kron_imag = tables
    sampled = (mask_item > 0)[:, :, None]
    initial = jnp.where(sampled, observed, jnp.zeros_like(observed)).astype(jnp.bfloat16)
    halfway = observed.shape[-1] // 2

    def forward(volume):
        middle = apply_along(kron_real, kron_imag, volume, 'kj,ajl->akl').astype(jnp.bfloat16)
        return apply_along(cos_table, sin_table, middle, 'ka,ajl->kjl')

    def inverse(volume):
        middle = apply_along(cos_table, -sin_table, volume, 'ka,ajl->kjl').astype(jnp.bfloat16)
        return apply_along(kron_real, -kron_imag, middle, 'kj,ajl->akl')

    def magnitude(coeffs):
        return jnp.sqrt(coeffs[..., :halfway] ** 2 + coeffs[..., halfway:] ** 2)
    largest = lax.optimization_barrier(jnp.max(magnitude(forward(initial)), axis=(0, 1)))

    def sweep_step(sweep, volume):
        coeffs = forward(volume)
        size_now = magnitude(coeffs)
        cutoff = largest * (0.5 * jnp.power(jnp.float32(0.6), sweep.astype(jnp.float32)))
        factor = jax.nn.relu(size_now - cutoff) / (jnp.maximum(size_now, cutoff) + 1e-06)
        thinned = (coeffs * jnp.concatenate([factor, factor], axis=-1)).astype(jnp.bfloat16)
        returned = inverse(thinned)
        return jnp.where(sampled, observed.astype(jnp.float32), returned).astype(jnp.bfloat16)
    return lax.fori_loop(0, sweeps, sweep_step, initial)

def reference(spectra, sampled_mask, counts):
    tables = dft_tables(SIDE)
    lane_count = 2 * FREQ
    patches = spectra.reshape(NAZ * P_AZ, SIDE, SIDE * SIDE, lane_count)
    masks = sampled_mask.reshape(NAZ * P_AZ, SIDE, SIDE * SIDE)
    sweeps = counts.reshape(NAZ * P_AZ)

    def run_patch(item):
        return project_patch(item[0], item[1], item[2], tables)
    result = lax.map(run_patch, (patches, masks, sweeps))
    result = result.reshape(NAZ, P_AZ, SIDE, SIDE * SIDE, lane_count)
    halfway = SIDE // 2
    own_half = result[:, :, :halfway].astype(jnp.float32)
    top_half = result[:, :, halfway:].astype(jnp.float32)
    earlier = jnp.concatenate([jnp.zeros((NAZ, 1, halfway, SIDE * SIDE, lane_count), jnp.float32), top_half[:, :-1]], axis=1)
    weight = ((jnp.arange(halfway, dtype=jnp.float32) + 0.5) / halfway)[:, None, None]
    blended = (weight * own_half + (1.0 - weight) * earlier).astype(jnp.bfloat16)
    return blended.reshape(NAZ, P_AZ, halfway * SIDE * SIDE, lane_count)
```

```python
import functools

import jax
import jax.numpy as jnp
from jax import lax
from jax.experimental import pallas as pl
from jax.experimental.pallas import tpu as pltpu
from jax.sharding import PartitionSpec as P


def passed_along(block, axis, distance):
    devices = range(lax.axis_size(axis))
    route = [(i - distance, i) for i in devices if i - distance in devices]
    return lax.ppermute(block, axis, route)


def dft_tables(extent):
    indices = jnp.arange(extent, dtype=jnp.int32)
    product = indices[:, None] * indices[None, :] % extent
    phase = product.astype(jnp.float32) * (2.0 * jnp.pi / extent)
    scale = extent ** (-0.5)
    cos_table = jnp.cos(phase) * scale
    sin_table = -jnp.sin(phase) * scale
    kron_real = jnp.kron(cos_table, cos_table) - jnp.kron(sin_table, sin_table)
    kron_imag = jnp.kron(cos_table, sin_table) + jnp.kron(sin_table, cos_table)
    return (
        cos_table.astype(jnp.bfloat16),
        sin_table.astype(jnp.bfloat16),
        kron_real.astype(jnp.bfloat16),
        kron_imag.astype(jnp.bfloat16),
    )


def kernel_tables(extent):
    cos_table, sin_table, kron_real, kron_imag = dft_tables(extent)
    eye = jnp.eye(extent, dtype=jnp.float32)

    def spread(table):
        return jnp.kron(table.astype(jnp.float32), eye).astype(jnp.bfloat16)

    return jnp.stack([
        jnp.concatenate([kron_real, kron_imag], axis=1),
        jnp.concatenate([kron_real, -kron_imag], axis=1),
        jnp.concatenate([spread(cos_table), spread(sin_table)], axis=1),
        jnp.concatenate([spread(cos_table), spread(-sin_table)], axis=1),
    ])


def pocs_kernel(counts_ref, scales_ref, obs_ref, mask_ref, tab_ref, out_ref, y_ref, v_ref):
    p = pl.program_id(0)
    extent = obs_ref.shape[1]
    lanes = obs_ref.shape[3]
    half = lanes // 2
    plane = obs_ref.shape[2]
    sweeps = counts_ref[p]
    lower = lax.broadcasted_iota(jnp.int32, (1, lanes), 1) < half

    def apply(table_idx, block):
        rolled = pltpu.roll(block, half, 1)
        rotated = jnp.where(lower, -rolled, rolled)
        stacked = jnp.concatenate([block, rotated], axis=0)
        return jnp.dot(tab_ref[table_idx], stacked, preferred_element_type=jnp.float32)

    def stage_one(a, volume):
        middle = apply(0, volume).astype(jnp.bfloat16)
        for hi in range(extent):
            y_ref[hi, a] = middle[hi * extent:(hi + 1) * extent]

    def magnitude(c):
        return jnp.sqrt(c * c + pltpu.roll(c, half, 1) ** 2)

    def init_a(a, carry):
        sampled = mask_ref[0, a] > 0
        initial = jnp.where(sampled, obs_ref[0, a], jnp.zeros_like(obs_ref[0, a]))
        out_ref[0, a] = initial
        stage_one(a, initial)
        return carry

    lax.fori_loop(0, extent, init_a, 0, unroll=16)

    def init_hi(hi, running):
        coeffs = apply(2, y_ref[hi].reshape(plane, lanes))
        return jnp.maximum(running, jnp.max(magnitude(coeffs), axis=0, keepdims=True))

    largest = lax.fori_loop(0, extent, init_hi, jnp.zeros((1, lanes), jnp.float32), unroll=16)

    def sweep_step(k, carry):
        cutoff = largest * scales_ref[k]

        def thin_hi(hi, c2):
            coeffs = apply(2, y_ref[hi].reshape(plane, lanes))
            size_now = magnitude(coeffs)
            factor = jnp.maximum(size_now - cutoff, 0.0) / (jnp.maximum(size_now, cutoff) + 1e-06)
            thinned = (coeffs * factor).astype(jnp.bfloat16)
            back_mid = apply(3, thinned).astype(jnp.bfloat16)
            for a in range(extent):
                v_ref[a, hi] = back_mid[a * extent:(a + 1) * extent]
            return c2

        lax.fori_loop(0, extent, thin_hi, 0, unroll=16)

        def back_a(a, c2):
            returned = apply(1, v_ref[a].reshape(plane, lanes))
            sampled = mask_ref[0, a] > 0
            updated = jnp.where(sampled, obs_ref[0, a].astype(jnp.float32), returned).astype(jnp.bfloat16)
            out_ref[0, a] = updated

            @pl.when(k + 1 < sweeps)
            def _():
                stage_one(a, updated)

            return c2

        lax.fori_loop(0, extent, back_a, 0, unroll=16)
        return carry

    lax.fori_loop(0, sweeps, sweep_step, 0)


def run_patches(observed, maskb, sweeps, scales, tables):
    count, extent, plane, lanes = observed.shape
    block = pl.BlockSpec((1, extent, plane, lanes), lambda p, c, s: (p, 0, 0, 0))
    grid_spec = pltpu.PrefetchScalarGridSpec(
        num_scalar_prefetch=2,
        grid=(count,),
        in_specs=[block, block, pl.BlockSpec(tables.shape, lambda p, c, s: (0, 0, 0))],
        out_specs=block,
        scratch_shapes=[
            pltpu.VMEM((extent, extent, extent, lanes), jnp.bfloat16),
            pltpu.VMEM((extent, extent, extent, lanes), jnp.bfloat16),
        ],
    )
    return pl.pallas_call(
        pocs_kernel,
        grid_spec=grid_spec,
        out_shape=jax.ShapeDtypeStruct(observed.shape, jnp.bfloat16),
        compiler_params=pltpu.CompilerParams(dimension_semantics=("arbitrary",)),
    )(sweeps, scales, observed, maskb, tables)


def shards(spectra, sampled_mask, counts):
    regrouped = lax.all_to_all(spectra, "shot", split_axis=1, concat_axis=2, tiled=True)
    owned_count = regrouped.shape[1]
    extent = sampled_mask.shape[2]
    plane = extent * extent
    lane_count = regrouped.shape[3]
    tables = kernel_tables(extent)
    observed = regrouped.reshape(owned_count, extent, plane, lane_count)
    maskb = jnp.broadcast_to((sampled_mask[0] > 0).astype(jnp.bfloat16)[..., None], observed.shape)
    sweeps = counts[0]
    steps = jnp.arange(8, dtype=jnp.float32)
    scales = 0.5 * jnp.power(jnp.float32(0.6), steps)

    result = run_patches(observed, maskb, sweeps, scales, tables)
    halfway = extent // 2
    arrived = passed_along(result[-1, halfway:], "shot", 1)
    earlier = jnp.concatenate([arrived[None], result[:-1, halfway:]], axis=0).astype(jnp.float32)
    weight = ((jnp.arange(halfway, dtype=jnp.float32) + 0.5) / halfway)[:, None, None]
    mixed = weight * result[:, :halfway].astype(jnp.float32) + (1.0 - weight) * earlier
    mixed = mixed.astype(jnp.bfloat16).reshape(1, owned_count, halfway * plane, lane_count)
    return lax.all_to_all(mixed, "shot", split_axis=2, concat_axis=1, tiled=True)


def solution(mesh):
    return jax.shard_map(
        shards,
        mesh=mesh,
        in_specs=(P("az", None, "shot", None), P("az", "shot", None, None), P("az", "shot")),
        out_specs=P("az", None, "shot", None),
        check_vma=False,
    )
```

```python
import jax
import jax.numpy as jnp
from jax import lax
from jax.experimental import pallas as pl
from jax.experimental.pallas import tpu as pltpu
from jax.sharding import PartitionSpec as P


def passed_along(block, axis, distance):
    devices = range(lax.axis_size(axis))
    route = [(i - distance, i) for i in devices if i - distance in devices]
    return lax.ppermute(block, axis, route)


def dft_tables(extent):
    indices = jnp.arange(extent, dtype=jnp.int32)
    product = indices[:, None] * indices[None, :] % extent
    phase = product.astype(jnp.float32) * (2.0 * jnp.pi / extent)
    scale = extent ** (-0.5)
    cos_table = jnp.cos(phase) * scale
    sin_table = -jnp.sin(phase) * scale
    kron_real = jnp.kron(cos_table, cos_table) - jnp.kron(sin_table, sin_table)
    kron_imag = jnp.kron(cos_table, sin_table) + jnp.kron(sin_table, cos_table)
    return (
        cos_table.astype(jnp.bfloat16),
        sin_table.astype(jnp.bfloat16),
        kron_real.astype(jnp.bfloat16),
        kron_imag.astype(jnp.bfloat16),
    )


def kernel_tables(extent):
    cos_table, sin_table, kron_real, kron_imag = dft_tables(extent)
    eye = jnp.eye(extent, dtype=jnp.float32)

    def spread(table):
        return jnp.kron(table.astype(jnp.float32), eye).astype(jnp.bfloat16)

    return jnp.stack([
        jnp.concatenate([kron_real, kron_imag], axis=1),
        jnp.concatenate([kron_real, -kron_imag], axis=1),
        jnp.concatenate([spread(cos_table), spread(sin_table)], axis=1),
        jnp.concatenate([spread(cos_table), spread(-sin_table)], axis=1),
    ])


def pocs_kernel(counts_ref, scales_ref, obs_ref, mask_ref, tab_ref, out_ref, y_ref, v_ref):
    p = pl.program_id(0)
    extent = obs_ref.shape[1]
    lanes = obs_ref.shape[3]
    half = lanes // 2
    plane = obs_ref.shape[2]
    half_axis = extent // 2
    sweeps = counts_ref[p]
    lower = lax.broadcasted_iota(jnp.int32, (1, lanes), 1) < half

    def apply(table_idx, block):
        rolled = pltpu.roll(block, half, 1)
        rotated = jnp.where(lower, -rolled, rolled)
        stacked = jnp.concatenate([block, rotated], axis=0)
        return jnp.dot(tab_ref[table_idx], stacked, preferred_element_type=jnp.float32)

    def stage_one(a, volume):
        middle = apply(0, volume).astype(jnp.bfloat16)
        for hi in range(extent):
            y_ref[hi, a] = middle[hi * extent:(hi + 1) * extent]

    def magnitude(c):
        return jnp.sqrt(c * c + pltpu.roll(c, half, 1) ** 2)

    def init_a(a, carry):
        sampled = mask_ref[0, a] > 0
        initial = jnp.where(sampled, obs_ref[0, a], jnp.zeros_like(obs_ref[0, a]))
        for quarter in range(4):
            rows = plane // 4
            out_ref[(a % half_axis) * 4 + quarter, 0, a // half_axis] = initial[quarter * rows:(quarter + 1) * rows]
        stage_one(a, initial)
        return carry

    lax.fori_loop(0, extent, init_a, 0, unroll=16)

    def init_hi(hi, running):
        coeffs = apply(2, y_ref[hi].reshape(plane, lanes))
        return jnp.maximum(running, jnp.max(magnitude(coeffs), axis=0, keepdims=True))

    largest = lax.fori_loop(0, extent, init_hi, jnp.zeros((1, lanes), jnp.float32), unroll=16)

    def sweep_step(k, carry):
        cutoff = largest * scales_ref[k]

        def thin_hi(hi, c2):
            coeffs = apply(2, y_ref[hi].reshape(plane, lanes))
            size_now = magnitude(coeffs)
            factor = jnp.maximum(size_now - cutoff, 0.0) / (jnp.maximum(size_now, cutoff) + 1e-06)
            thinned = (coeffs * factor).astype(jnp.bfloat16)
            back_mid = apply(3, thinned).astype(jnp.bfloat16)
            for a in range(extent):
                v_ref[a, hi] = back_mid[a * extent:(a + 1) * extent]
            return c2

        lax.fori_loop(0, extent, thin_hi, 0, unroll=16)

        def back_a(a, c2):
            returned = apply(1, v_ref[a].reshape(plane, lanes))
            sampled = mask_ref[0, a] > 0
            updated = jnp.where(sampled, obs_ref[0, a].astype(jnp.float32), returned).astype(jnp.bfloat16)
            for quarter in range(4):
                rows = plane // 4
                out_ref[(a % half_axis) * 4 + quarter, 0, a // half_axis] = updated[quarter * rows:(quarter + 1) * rows]

            @pl.when(k + 1 < sweeps)
            def _():
                stage_one(a, updated)

            return c2

        lax.fori_loop(0, extent, back_a, 0, unroll=16)
        return carry

    lax.fori_loop(0, sweeps, sweep_step, 0)


def run_patches(observed, maskb, sweeps, scales, tables):
    count, extent, plane, lanes = observed.shape
    block = pl.BlockSpec((1, extent, plane, lanes), lambda p, c, s: (p, 0, 0, 0))
    dests = extent // 2 * 4
    out_block = pl.BlockSpec((dests, 1, 2, plane // 4, lanes), lambda p, c, s: (0, p, 0, 0, 0))
    grid_spec = pltpu.PrefetchScalarGridSpec(
        num_scalar_prefetch=2,
        grid=(count,),
        in_specs=[block, block, pl.BlockSpec(tables.shape, lambda p, c, s: (0, 0, 0))],
        out_specs=out_block,
        scratch_shapes=[
            pltpu.VMEM((extent, extent, extent, lanes), jnp.bfloat16),
            pltpu.VMEM((extent, extent, extent, lanes), jnp.bfloat16),
        ],
    )
    return pl.pallas_call(
        pocs_kernel,
        grid_spec=grid_spec,
        out_shape=jax.ShapeDtypeStruct((dests, count, 2, plane // 4, lanes), jnp.bfloat16),
        compiler_params=pltpu.CompilerParams(dimension_semantics=("arbitrary",)),
    )(sweeps, scales, observed, maskb, tables)


def snake_slots(devices, per_device):
    ranks = []
    for d in range(devices):
        for i in range(per_device):
            ranks.append(i * devices + (d if i % 2 == 0 else devices - 1 - d))
    return jnp.array(ranks, jnp.int32)


def shards(spectra, sampled_mask, counts):
    devices = lax.axis_size("shot")
    me = lax.axis_index("shot")
    owned_count = counts.shape[1]
    total = devices * owned_count
    extent = sampled_mask.shape[2]
    plane = extent * extent
    lane_count = spectra.shape[3]
    halfway = extent // 2

    all_counts = lax.all_gather(counts[0], "shot", tiled=True)
    order = jnp.argsort(-all_counts, stable=True).astype(jnp.int32)
    perm = order[snake_slots(devices, owned_count)]
    inverse = jnp.zeros((total,), jnp.int32).at[perm].set(jnp.arange(total, dtype=jnp.int32))
    mine = lax.dynamic_slice(perm, (me * owned_count,), (owned_count,))

    routed = jnp.take(spectra, perm, axis=1)
    regrouped = lax.all_to_all(routed, "shot", split_axis=1, concat_axis=2, tiled=True)
    observed = regrouped.reshape(owned_count, extent, plane, lane_count)
    all_masks = lax.all_gather((sampled_mask[0] > 0).astype(jnp.bfloat16), "shot", tiled=True)
    masks = jnp.take(all_masks, mine, axis=0)
    maskb = jnp.broadcast_to(masks[..., None], observed.shape)
    sweeps = jnp.take(all_counts, mine)
    tables = kernel_tables(extent)
    steps = jnp.arange(8, dtype=jnp.float32)
    scales = 0.5 * jnp.power(jnp.float32(0.6), steps)

    result = run_patches(observed, maskb, sweeps, scales, tables)
    back = lax.all_to_all(result, "shot", split_axis=0, concat_axis=1, tiled=True)[0]
    back = jnp.take(back, inverse, axis=0)
    own_half = back[:, 0].astype(jnp.float32)
    top_half = back[:, 1].astype(jnp.float32)
    earlier = jnp.concatenate([jnp.zeros_like(top_half[:1]), top_half[:-1]], axis=0)
    h = (me // (devices // halfway)).astype(jnp.float32)
    weight = (h + 0.5) / halfway
    mixed = weight * own_half + (1.0 - weight) * earlier
    return mixed.astype(jnp.bfloat16)[None]


def solution(mesh):
    return jax.shard_map(
        shards,
        mesh=mesh,
        in_specs=(P("az", None, "shot", None), P("az", "shot", None, None), P("az", "shot")),
        out_specs=P("az", None, "shot", None),
        check_vma=False,
    )
```

```python
import jax
import jax.numpy as jnp
from jax import lax
from jax.experimental import pallas as pl
from jax.experimental.pallas import tpu as pltpu
from jax.sharding import PartitionSpec as P


def passed_along(block, axis, distance):
    devices = range(lax.axis_size(axis))
    route = [(i - distance, i) for i in devices if i - distance in devices]
    return lax.ppermute(block, axis, route)


def dft_tables(extent):
    indices = jnp.arange(extent, dtype=jnp.int32)
    product = indices[:, None] * indices[None, :] % extent
    phase = product.astype(jnp.float32) * (2.0 * jnp.pi / extent)
    scale = extent ** (-0.5)
    cos_table = jnp.cos(phase) * scale
    sin_table = -jnp.sin(phase) * scale
    kron_real = jnp.kron(cos_table, cos_table) - jnp.kron(sin_table, sin_table)
    kron_imag = jnp.kron(cos_table, sin_table) + jnp.kron(sin_table, cos_table)
    return (
        cos_table.astype(jnp.bfloat16),
        sin_table.astype(jnp.bfloat16),
        kron_real.astype(jnp.bfloat16),
        kron_imag.astype(jnp.bfloat16),
    )


def kernel_tables(extent):
    cos_table, sin_table, kron_real, kron_imag = dft_tables(extent)
    eye = jnp.eye(extent, dtype=jnp.float32)

    def spread(table):
        return jnp.kron(table.astype(jnp.float32), eye).astype(jnp.bfloat16)

    return jnp.stack([
        jnp.concatenate([kron_real, kron_imag], axis=1),
        jnp.concatenate([kron_real, -kron_imag], axis=1),
        jnp.concatenate([spread(cos_table), spread(sin_table)], axis=1),
        jnp.concatenate([spread(cos_table), spread(-sin_table)], axis=1),
    ])


def pocs_kernel(counts_ref, scales_ref, obs_ref, tab_ref, out_ref, y_ref, v_ref):
    p = pl.program_id(0)
    extent = obs_ref.shape[1]
    lanes = obs_ref.shape[3]
    half = lanes // 2
    plane = obs_ref.shape[2]
    half_axis = extent // 2
    sweeps = counts_ref[p]
    lower = lax.broadcasted_iota(jnp.int32, (1, lanes), 1) < half

    def apply(table_idx, block):
        rolled = pltpu.roll(block, half, 1)
        rotated = jnp.where(lower, -rolled, rolled)
        stacked = jnp.concatenate([block, rotated], axis=0)
        return jnp.dot(tab_ref[table_idx], stacked, preferred_element_type=jnp.float32)

    def stage_one(a, volume):
        middle = apply(0, volume).astype(jnp.bfloat16)
        for hi in range(extent):
            y_ref[hi, a] = middle[hi * extent:(hi + 1) * extent]

    def recorded(v):
        wide = v.astype(jnp.float32)
        return wide == wide

    def magnitude(c):
        return jnp.sqrt(c * c + pltpu.roll(c, half, 1) ** 2)

    def init_a(a, carry):
        observed = obs_ref[0, a]
        sampled = recorded(observed)
        initial = jnp.where(sampled, observed, jnp.zeros_like(observed))
        for quarter in range(4):
            rows = plane // 4
            out_ref[(a % half_axis) * 4 + quarter, 0, a // half_axis] = initial[quarter * rows:(quarter + 1) * rows]
        stage_one(a, initial)
        return carry

    lax.fori_loop(0, extent, init_a, 0, unroll=16)

    def init_hi(hi, running):
        coeffs = apply(2, y_ref[hi].reshape(plane, lanes))
        return jnp.maximum(running, jnp.max(magnitude(coeffs), axis=0, keepdims=True))

    largest = lax.fori_loop(0, extent, init_hi, jnp.zeros((1, lanes), jnp.float32), unroll=16)

    def sweep_step(k, carry):
        cutoff = largest * scales_ref[k]

        def thin_hi(hi, c2):
            coeffs = apply(2, y_ref[hi].reshape(plane, lanes))
            size_now = magnitude(coeffs)
            factor = jnp.maximum(size_now - cutoff, 0.0) / (jnp.maximum(size_now, cutoff) + 1e-06)
            thinned = (coeffs * factor).astype(jnp.bfloat16)
            back_mid = apply(3, thinned).astype(jnp.bfloat16)
            for a in range(extent):
                v_ref[a, hi] = back_mid[a * extent:(a + 1) * extent]
            return c2

        lax.fori_loop(0, extent, thin_hi, 0, unroll=16)

        def back_a(a, c2):
            returned = apply(1, v_ref[a].reshape(plane, lanes))
            observed = obs_ref[0, a].astype(jnp.float32)
            updated = jnp.where(observed == observed, observed, returned).astype(jnp.bfloat16)
            for quarter in range(4):
                rows = plane // 4
                out_ref[(a % half_axis) * 4 + quarter, 0, a // half_axis] = updated[quarter * rows:(quarter + 1) * rows]

            @pl.when(k + 1 < sweeps)
            def _():
                stage_one(a, updated)

            return c2

        lax.fori_loop(0, extent, back_a, 0, unroll=16)
        return carry

    lax.fori_loop(0, sweeps, sweep_step, 0)


def run_patches(observed, sweeps, scales, tables):
    count, extent, plane, lanes = observed.shape
    block = pl.BlockSpec((1, extent, plane, lanes), lambda p, c, s: (p, 0, 0, 0))
    dests = extent // 2 * 4
    out_block = pl.BlockSpec((dests, 1, 2, plane // 4, lanes), lambda p, c, s: (0, p, 0, 0, 0))
    grid_spec = pltpu.PrefetchScalarGridSpec(
        num_scalar_prefetch=2,
        grid=(count,),
        in_specs=[block, pl.BlockSpec(tables.shape, lambda p, c, s: (0, 0, 0))],
        out_specs=out_block,
        scratch_shapes=[
            pltpu.VMEM((extent, extent, extent, lanes), jnp.bfloat16),
            pltpu.VMEM((extent, extent, extent, lanes), jnp.bfloat16),
        ],
    )
    return pl.pallas_call(
        pocs_kernel,
        grid_spec=grid_spec,
        out_shape=jax.ShapeDtypeStruct((dests, count, 2, plane // 4, lanes), jnp.bfloat16),
        compiler_params=pltpu.CompilerParams(dimension_semantics=("arbitrary",)),
    )(sweeps, scales, observed, tables)


def snake_slots(devices, per_device):
    ranks = []
    for d in range(devices):
        for i in range(per_device):
            ranks.append(i * devices + (d if i % 2 == 0 else devices - 1 - d))
    return jnp.array(ranks, jnp.int32)


def shards(spectra, sampled_mask, counts):
    devices = lax.axis_size("shot")
    me = lax.axis_index("shot")
    owned_count = counts.shape[1]
    total = devices * owned_count
    extent = sampled_mask.shape[2]
    plane = extent * extent
    lane_count = spectra.shape[3]
    halfway = extent // 2

    mask_rows = (sampled_mask[0] > 0).astype(jnp.bfloat16).reshape(owned_count, devices, -1)
    count_cols = jnp.broadcast_to(counts[0].astype(jnp.bfloat16)[:, None, None], (owned_count, devices, 8))
    packed = jnp.concatenate([mask_rows, count_cols], axis=2)[None]
    arrived = lax.all_to_all(packed, "shot", split_axis=2, concat_axis=1, tiled=True)[0, :, 0]
    local_traces = spectra.shape[2]
    local_mask = arrived[:, :local_traces]
    all_counts = arrived[:, local_traces].astype(jnp.int32)

    order = jnp.argsort(-all_counts, stable=True).astype(jnp.int32)
    perm = order[snake_slots(devices, owned_count)]
    inverse = jnp.zeros((total,), jnp.int32).at[perm].set(jnp.arange(total, dtype=jnp.int32))
    mine = lax.dynamic_slice(perm, (me * owned_count,), (owned_count,))

    marked = jnp.where(local_mask[None, :, :, None] > 0, spectra, jnp.nan).astype(spectra.dtype)
    routed = jnp.take(marked, perm, axis=1)
    regrouped = lax.all_to_all(routed, "shot", split_axis=1, concat_axis=2, tiled=True)
    observed = regrouped.reshape(owned_count, extent, plane, lane_count)
    sweeps = jnp.take(all_counts, mine)
    tables = kernel_tables(extent)
    steps = jnp.arange(8, dtype=jnp.float32)
    scales = 0.5 * jnp.power(jnp.float32(0.6), steps)

    result = run_patches(observed, sweeps, scales, tables)
    back = lax.all_to_all(result, "shot", split_axis=0, concat_axis=1, tiled=True)[0]
    back = jnp.take(back, inverse, axis=0)
    own_half = back[:, 0].astype(jnp.float32)
    top_half = back[:, 1].astype(jnp.float32)
    earlier = jnp.concatenate([jnp.zeros_like(top_half[:1]), top_half[:-1]], axis=0)
    h = (me // (devices // halfway)).astype(jnp.float32)
    weight = (h + 0.5) / halfway
    mixed = weight * own_half + (1.0 - weight) * earlier
    return mixed.astype(jnp.bfloat16)[None]


def solution(mesh):
    return jax.shard_map(
        shards,
        mesh=mesh,
        in_specs=(P("az", None, "shot", None), P("az", "shot", None, None), P("az", "shot")),
        out_specs=P("az", None, "shot", None),
        check_vma=False,
    )
```

```python
import jax
import jax.numpy as jnp
from jax import lax
from jax.experimental import pallas as pl
from jax.experimental.pallas import tpu as pltpu
from jax.sharding import PartitionSpec as P


def passed_along(block, axis, distance):
    devices = range(lax.axis_size(axis))
    route = [(i - distance, i) for i in devices if i - distance in devices]
    return lax.ppermute(block, axis, route)


def dft_tables(extent):
    indices = jnp.arange(extent, dtype=jnp.int32)
    product = indices[:, None] * indices[None, :] % extent
    phase = product.astype(jnp.float32) * (2.0 * jnp.pi / extent)
    scale = extent ** (-0.5)
    cos_table = jnp.cos(phase) * scale
    sin_table = -jnp.sin(phase) * scale
    kron_real = jnp.kron(cos_table, cos_table) - jnp.kron(sin_table, sin_table)
    kron_imag = jnp.kron(cos_table, sin_table) + jnp.kron(sin_table, cos_table)
    return (
        cos_table.astype(jnp.bfloat16),
        sin_table.astype(jnp.bfloat16),
        kron_real.astype(jnp.bfloat16),
        kron_imag.astype(jnp.bfloat16),
    )


def kernel_tables(extent):
    cos_table, sin_table, kron_real, kron_imag = dft_tables(extent)
    eye = jnp.eye(extent, dtype=jnp.float32)

    def spread(table):
        return jnp.kron(table.astype(jnp.float32), eye).astype(jnp.bfloat16)

    return jnp.stack([
        jnp.concatenate([kron_real, kron_imag], axis=1),
        jnp.concatenate([kron_real, -kron_imag], axis=1),
        jnp.concatenate([spread(cos_table), spread(sin_table)], axis=1),
        jnp.concatenate([spread(cos_table), spread(-sin_table)], axis=1),
    ])


def pocs_kernel(counts_ref, scales_ref, obs_ref, tab_ref, out_ref, y_ref, v_ref):
    p = pl.program_id(0)
    extent = obs_ref.shape[1]
    lanes = obs_ref.shape[3]
    half = lanes // 2
    plane = obs_ref.shape[2]
    half_axis = extent // 2
    sweeps = counts_ref[p]
    lower = lax.broadcasted_iota(jnp.int32, (1, lanes), 1) < half

    def apply(table_idx, block):
        rolled = pltpu.roll(block, half, 1)
        rotated = jnp.where(lower, -rolled, rolled)
        stacked = jnp.concatenate([block, rotated], axis=0)
        return jnp.dot(tab_ref[table_idx], stacked, preferred_element_type=jnp.float32)

    def stage_one(a, volume):
        middle = apply(0, volume).astype(jnp.bfloat16)
        for hi in range(extent):
            y_ref[hi, a] = middle[hi * extent:(hi + 1) * extent]

    def recorded(v):
        wide = v.astype(jnp.float32)
        return wide == wide

    def magnitude(c):
        return jnp.sqrt(c * c + pltpu.roll(c, half, 1) ** 2)

    def init_a(a, carry):
        observed = obs_ref[0, a]
        sampled = recorded(observed)
        initial = jnp.where(sampled, observed, jnp.zeros_like(observed))
        for quarter in range(4):
            rows = plane // 4
            out_ref[(a % half_axis) * 4 + quarter, 0, a // half_axis] = initial[quarter * rows:(quarter + 1) * rows]
        stage_one(a, initial)
        return carry

    lax.fori_loop(0, extent, init_a, 0, unroll=16)

    def init_hi(hi, running):
        coeffs = apply(2, y_ref[hi].reshape(plane, lanes))
        return jnp.maximum(running, jnp.max(magnitude(coeffs), axis=0, keepdims=True))

    largest = lax.fori_loop(0, extent, init_hi, jnp.zeros((1, lanes), jnp.float32), unroll=16)

    def sweep_step(k, carry):
        cutoff = largest * scales_ref[k]

        def thin_hi(hi, c2):
            coeffs = apply(2, y_ref[hi].reshape(plane, lanes))
            size_now = magnitude(coeffs)
            factor = jnp.maximum(size_now - cutoff, 0.0) / (jnp.maximum(size_now, cutoff) + 1e-06)
            thinned = (coeffs * factor).astype(jnp.bfloat16)
            back_mid = apply(3, thinned).astype(jnp.bfloat16)
            for a in range(extent):
                v_ref[a, hi] = back_mid[a * extent:(a + 1) * extent]
            return c2

        lax.fori_loop(0, extent, thin_hi, 0, unroll=16)

        def back_a(a, c2):
            returned = apply(1, v_ref[a].reshape(plane, lanes))
            observed = obs_ref[0, a].astype(jnp.float32)
            updated = jnp.where(observed == observed, observed, returned).astype(jnp.bfloat16)
            for quarter in range(4):
                rows = plane // 4
                out_ref[(a % half_axis) * 4 + quarter, 0, a // half_axis] = updated[quarter * rows:(quarter + 1) * rows]

            @pl.when(k + 1 < sweeps)
            def _():
                stage_one(a, updated)

            return c2

        lax.fori_loop(0, extent, back_a, 0, unroll=16)
        return carry

    lax.fori_loop(0, sweeps, sweep_step, 0)


def run_patches(observed, sweeps, scales, tables):
    count, extent, plane, lanes = observed.shape
    block = pl.BlockSpec((1, extent, plane, lanes), lambda p, c, s: (p, 0, 0, 0))
    dests = extent // 2 * 4
    out_block = pl.BlockSpec((dests, 1, 2, plane // 4, lanes), lambda p, c, s: (0, p, 0, 0, 0))
    grid_spec = pltpu.PrefetchScalarGridSpec(
        num_scalar_prefetch=2,
        grid=(count,),
        in_specs=[block, pl.BlockSpec(tables.shape, lambda p, c, s: (0, 0, 0))],
        out_specs=out_block,
        scratch_shapes=[
            pltpu.VMEM((extent, extent, extent, lanes), jnp.bfloat16),
            pltpu.VMEM((extent, extent, extent, lanes), jnp.bfloat16),
        ],
    )
    return pl.pallas_call(
        pocs_kernel,
        grid_spec=grid_spec,
        out_shape=jax.ShapeDtypeStruct((dests, count, 2, plane // 4, lanes), jnp.bfloat16),
        compiler_params=pltpu.CompilerParams(dimension_semantics=("arbitrary",)),
    )(sweeps, scales, observed, tables)


def snake_slots(devices, per_device):
    ranks = []
    for d in range(devices):
        for i in range(per_device):
            ranks.append(i * devices + (d if i % 2 == 0 else devices - 1 - d))
    return jnp.array(ranks, jnp.int32)


def shards(spectra, sampled_mask, counts):
    devices = lax.axis_size("shot")
    me = lax.axis_index("shot")
    owned_count = counts.shape[1]
    total = devices * owned_count
    extent = sampled_mask.shape[2]
    plane = extent * extent
    lane_count = spectra.shape[3]
    halfway = extent // 2

    mask_rows = (sampled_mask[0] > 0).astype(jnp.bfloat16).reshape(owned_count, devices, -1)
    count_cols = jnp.broadcast_to(counts[0].astype(jnp.bfloat16)[:, None, None], (owned_count, devices, 8))
    packed = jnp.concatenate([mask_rows, count_cols], axis=2)[None]
    arrived = lax.all_to_all(packed, "shot", split_axis=2, concat_axis=1, tiled=True)[0, :, 0]
    local_traces = spectra.shape[2]
    local_mask = arrived[:, :local_traces]
    all_counts = arrived[:, local_traces].astype(jnp.int32)

    order = jnp.argsort(-all_counts, stable=True).astype(jnp.int32)
    perm = order[snake_slots(devices, owned_count)]
    inverse = jnp.zeros((total,), jnp.int32).at[perm].set(jnp.arange(total, dtype=jnp.int32))
    mine = lax.dynamic_slice(perm, (me * owned_count,), (owned_count,))

    marked = jnp.where(local_mask[None, :, :, None] > 0, spectra, jnp.nan).astype(spectra.dtype)
    tables = kernel_tables(extent)
    steps = jnp.arange(8, dtype=jnp.float32)
    scales = 0.5 * jnp.power(jnp.float32(0.6), steps)
    slots = perm.reshape(devices, owned_count)
    sweeps = jnp.take(all_counts, mine)

    returned = []
    for slot in range(owned_count):
        routed = jnp.take(marked, slots[:, slot], axis=1)
        regrouped = lax.all_to_all(routed, "shot", split_axis=1, concat_axis=2, tiled=True)
        observed = regrouped.reshape(1, extent, plane, lane_count)
        result = run_patches(observed, sweeps[slot:slot + 1], scales, tables)
        returned.append(lax.all_to_all(result, "shot", split_axis=0, concat_axis=1, tiled=True)[0])
    back = jnp.stack(returned, axis=1).reshape((total,) + returned[0].shape[1:])
    back = jnp.take(back, inverse, axis=0)
    own_half = back[:, 0].astype(jnp.float32)
    top_half = back[:, 1].astype(jnp.float32)
    earlier = jnp.concatenate([jnp.zeros_like(top_half[:1]), top_half[:-1]], axis=0)
    h = (me // (devices // halfway)).astype(jnp.float32)
    weight = (h + 0.5) / halfway
    mixed = weight * own_half + (1.0 - weight) * earlier
    return mixed.astype(jnp.bfloat16)[None]


def solution(mesh):
    return jax.shard_map(
        shards,
        mesh=mesh,
        in_specs=(P("az", None, "shot", None), P("az", "shot", None, None), P("az", "shot")),
        out_specs=P("az", None, "shot", None),
        check_vma=False,
    )
```

```python
import jax
import jax.numpy as jnp
from jax import lax
from jax.experimental import pallas as pl
from jax.experimental.pallas import tpu as pltpu
from jax.sharding import PartitionSpec as P


def passed_along(block, axis, distance):
    devices = range(lax.axis_size(axis))
    route = [(i - distance, i) for i in devices if i - distance in devices]
    return lax.ppermute(block, axis, route)


def dft_tables(extent):
    indices = jnp.arange(extent, dtype=jnp.int32)
    product = indices[:, None] * indices[None, :] % extent
    phase = product.astype(jnp.float32) * (2.0 * jnp.pi / extent)
    scale = extent ** (-0.5)
    cos_table = jnp.cos(phase) * scale
    sin_table = -jnp.sin(phase) * scale
    kron_real = jnp.kron(cos_table, cos_table) - jnp.kron(sin_table, sin_table)
    kron_imag = jnp.kron(cos_table, sin_table) + jnp.kron(sin_table, cos_table)
    return (
        cos_table.astype(jnp.bfloat16),
        sin_table.astype(jnp.bfloat16),
        kron_real.astype(jnp.bfloat16),
        kron_imag.astype(jnp.bfloat16),
    )


def kernel_tables(extent):
    cos_table, sin_table, kron_real, kron_imag = dft_tables(extent)
    eye = jnp.eye(extent, dtype=jnp.float32)

    def spread(table):
        return jnp.kron(table.astype(jnp.float32), eye).astype(jnp.bfloat16)

    return jnp.stack([
        jnp.concatenate([kron_real, kron_imag], axis=1),
        jnp.concatenate([kron_real, -kron_imag], axis=1),
        jnp.concatenate([spread(cos_table), spread(sin_table)], axis=1),
        jnp.concatenate([spread(cos_table), spread(-sin_table)], axis=1),
    ])


GROUP = 16


def pocs_kernel(counts_ref, scales_ref, obs_ref, tab_ref, out_ref, y_ref, v_ref):
    p = pl.program_id(0)
    extent = obs_ref.shape[1]
    lanes = obs_ref.shape[3]
    half = lanes // 2
    plane = obs_ref.shape[2]
    half_axis = extent // 2
    rows = plane // 4
    group = GROUP
    groups = extent // group
    sweeps = counts_ref[p]
    lower = lax.broadcasted_iota(jnp.int32, (1, lanes), 1) < half

    def rot(block):
        rolled = pltpu.roll(block, half, 1)
        return jnp.where(lower, -rolled, rolled)

    def apply(table_idx, blocks):
        stacked = jnp.concatenate([
            jnp.concatenate(blocks, axis=1),
            jnp.concatenate([rot(b) for b in blocks], axis=1),
        ], axis=0)
        wide = jnp.dot(tab_ref[table_idx], stacked, preferred_element_type=jnp.float32)
        return [wide[:, g * lanes:(g + 1) * lanes] for g in range(len(blocks))]

    def scatter_y(a, middle):
        for hi in range(extent):
            y_ref[hi, a] = middle[hi * extent:(hi + 1) * extent]

    def stage_one(a0, blocks):
        for g, m in enumerate(apply(0, blocks)):
            scatter_y(a0 + g, m.astype(jnp.bfloat16))

    def write_out(a, value):
        for quarter in range(4):
            out_ref[(a % half_axis) * 4 + quarter, 0, a // half_axis] = value[quarter * rows:(quarter + 1) * rows]

    def recorded(v):
        wide = v.astype(jnp.float32)
        return wide == wide

    def magnitude(c):
        return jnp.sqrt(c * c + pltpu.roll(c, half, 1) ** 2)

    def init_group(i, carry):
        a0 = group * i
        initial = []
        for g in range(group):
            observed = obs_ref[0, a0 + g]
            value = jnp.where(recorded(observed), observed, jnp.zeros_like(observed))
            write_out(a0 + g, value)
            initial.append(value)
        stage_one(a0, initial)
        return carry

    lax.fori_loop(0, groups, init_group, 0, unroll=groups)

    def coeff_group(i):
        hi0 = group * i
        return apply(2, [y_ref[hi0 + g].reshape(plane, lanes) for g in range(group)])

    def init_hi(i, running):
        for coeffs in coeff_group(i):
            running = jnp.maximum(running, jnp.max(magnitude(coeffs), axis=0, keepdims=True))
        return running

    largest = lax.fori_loop(0, groups, init_hi, jnp.zeros((1, lanes), jnp.float32), unroll=groups)

    def sweep_step(k, carry):
        cutoff = largest * scales_ref[k]

        def thin_group(i, c2):
            thinned = []
            for coeffs in coeff_group(i):
                size_now = magnitude(coeffs)
                factor = jnp.maximum(size_now - cutoff, 0.0) / (jnp.maximum(size_now, cutoff) + 1e-06)
                thinned.append((coeffs * factor).astype(jnp.bfloat16))
            hi0 = group * i
            for g, back_mid in enumerate(apply(3, thinned)):
                back_mid = back_mid.astype(jnp.bfloat16)
                for a in range(extent):
                    v_ref[a, hi0 + g] = back_mid[a * extent:(a + 1) * extent]
            return c2

        lax.fori_loop(0, groups, thin_group, 0, unroll=groups)

        def back_group(i, c2):
            a0 = group * i
            returned = apply(1, [v_ref[a0 + g].reshape(plane, lanes) for g in range(group)])
            updated = []
            for g in range(group):
                observed = obs_ref[0, a0 + g].astype(jnp.float32)
                value = jnp.where(observed == observed, observed, returned[g]).astype(jnp.bfloat16)
                write_out(a0 + g, value)
                updated.append(value)

            @pl.when(k + 1 < sweeps)
            def _():
                stage_one(a0, updated)

            return c2

        lax.fori_loop(0, groups, back_group, 0, unroll=groups)
        return carry

    lax.fori_loop(0, sweeps, sweep_step, 0)


def run_patches(observed, sweeps, scales, tables):
    count, extent, plane, lanes = observed.shape
    block = pl.BlockSpec((1, extent, plane, lanes), lambda p, c, s: (p, 0, 0, 0))
    dests = extent // 2 * 4
    out_block = pl.BlockSpec((dests, 1, 2, plane // 4, lanes), lambda p, c, s: (0, p, 0, 0, 0))
    grid_spec = pltpu.PrefetchScalarGridSpec(
        num_scalar_prefetch=2,
        grid=(count,),
        in_specs=[block, pl.BlockSpec(tables.shape, lambda p, c, s: (0, 0, 0))],
        out_specs=out_block,
        scratch_shapes=[
            pltpu.VMEM((extent, extent, extent, lanes), jnp.bfloat16),
            pltpu.VMEM((extent, extent, extent, lanes), jnp.bfloat16),
        ],
    )
    return pl.pallas_call(
        pocs_kernel,
        grid_spec=grid_spec,
        out_shape=jax.ShapeDtypeStruct((dests, count, 2, plane // 4, lanes), jnp.bfloat16),
        compiler_params=pltpu.CompilerParams(dimension_semantics=("arbitrary",)),
    )(sweeps, scales, observed, tables)


def snake_slots(devices, per_device):
    ranks = []
    for d in range(devices):
        for i in range(per_device):
            ranks.append(i * devices + (d if i % 2 == 0 else devices - 1 - d))
    return jnp.array(ranks, jnp.int32)


def shards(spectra, sampled_mask, counts):
    devices = lax.axis_size("shot")
    me = lax.axis_index("shot")
    owned_count = counts.shape[1]
    total = devices * owned_count
    extent = sampled_mask.shape[2]
    plane = extent * extent
    lane_count = spectra.shape[3]
    halfway = extent // 2

    mask_rows = (sampled_mask[0] > 0).astype(jnp.bfloat16).reshape(owned_count, devices, -1)
    count_cols = jnp.broadcast_to(counts[0].astype(jnp.bfloat16)[:, None, None], (owned_count, devices, 8))
    packed = jnp.concatenate([mask_rows, count_cols], axis=2)[None]
    arrived = lax.all_to_all(packed, "shot", split_axis=2, concat_axis=1, tiled=True)[0, :, 0]
    local_traces = spectra.shape[2]
    local_mask = arrived[:, :local_traces]
    all_counts = arrived[:, local_traces].astype(jnp.int32)

    order = jnp.argsort(-all_counts, stable=True).astype(jnp.int32)
    perm = order[snake_slots(devices, owned_count)]
    inverse = jnp.zeros((total,), jnp.int32).at[perm].set(jnp.arange(total, dtype=jnp.int32))
    mine = lax.dynamic_slice(perm, (me * owned_count,), (owned_count,))

    marked = jnp.where(local_mask[None, :, :, None] > 0, spectra, jnp.nan).astype(spectra.dtype)
    routed = jnp.take(marked, perm, axis=1)
    regrouped = lax.all_to_all(routed, "shot", split_axis=1, concat_axis=2, tiled=True)
    observed = regrouped.reshape(owned_count, extent, plane, lane_count)
    sweeps = jnp.take(all_counts, mine)
    tables = kernel_tables(extent)
    steps = jnp.arange(8, dtype=jnp.float32)
    scales = 0.5 * jnp.power(jnp.float32(0.6), steps)

    result = run_patches(observed, sweeps, scales, tables)
    back = lax.all_to_all(result, "shot", split_axis=0, concat_axis=1, tiled=True)[0]
    back = jnp.take(back, inverse, axis=0)
    own_half = back[:, 0].astype(jnp.float32)
    top_half = back[:, 1].astype(jnp.float32)
    earlier = jnp.concatenate([jnp.zeros_like(top_half[:1]), top_half[:-1]], axis=0)
    h = (me // (devices // halfway)).astype(jnp.float32)
    weight = (h + 0.5) / halfway
    mixed = weight * own_half + (1.0 - weight) * earlier
    return mixed.astype(jnp.bfloat16)[None]


def solution(mesh):
    return jax.shard_map(
        shards,
        mesh=mesh,
        in_specs=(P("az", None, "shot", None), P("az", "shot", None, None), P("az", "shot")),
        out_specs=P("az", None, "shot", None),
        check_vma=False,
    )
```

```python
import jax
import jax.numpy as jnp
from jax import lax
from jax.experimental import pallas as pl
from jax.experimental.pallas import tpu as pltpu
from jax.sharding import PartitionSpec as P


def passed_along(block, axis, distance):
    devices = range(lax.axis_size(axis))
    route = [(i - distance, i) for i in devices if i - distance in devices]
    return lax.ppermute(block, axis, route)


def dft_tables(extent):
    indices = jnp.arange(extent, dtype=jnp.int32)
    product = indices[:, None] * indices[None, :] % extent
    phase = product.astype(jnp.float32) * (2.0 * jnp.pi / extent)
    scale = extent ** (-0.5)
    cos_table = jnp.cos(phase) * scale
    sin_table = -jnp.sin(phase) * scale
    kron_real = jnp.kron(cos_table, cos_table) - jnp.kron(sin_table, sin_table)
    kron_imag = jnp.kron(cos_table, sin_table) + jnp.kron(sin_table, cos_table)
    return (
        cos_table.astype(jnp.bfloat16),
        sin_table.astype(jnp.bfloat16),
        kron_real.astype(jnp.bfloat16),
        kron_imag.astype(jnp.bfloat16),
    )


def kernel_tables(extent):
    cos_table, sin_table, kron_real, kron_imag = dft_tables(extent)
    eye = jnp.eye(extent, dtype=jnp.float32)

    def spread(table):
        return jnp.kron(table.astype(jnp.float32), eye).astype(jnp.bfloat16)

    return jnp.stack([
        jnp.concatenate([kron_real, kron_imag], axis=1),
        jnp.concatenate([kron_real, -kron_imag], axis=1),
        jnp.concatenate([spread(cos_table), spread(sin_table)], axis=1),
        jnp.concatenate([spread(cos_table), spread(-sin_table)], axis=1),
    ])


GROUP = 16


def pocs_kernel(counts_ref, scales_ref, obs_ref, tab_ref, out_ref, y_ref, v_ref):
    p = pl.program_id(0)
    extent = obs_ref.shape[1]
    lanes = obs_ref.shape[3]
    half = lanes // 2
    plane = obs_ref.shape[2]
    half_axis = extent // 2
    rows = plane // 4
    group = GROUP
    groups = extent // group
    sweeps = counts_ref[p]
    lower = lax.broadcasted_iota(jnp.int32, (1, lanes), 1) < half

    def rot(block):
        rolled = pltpu.roll(block, half, 1)
        return jnp.where(lower, -rolled, rolled)

    def apply(table_idx, blocks):
        stacked = jnp.concatenate([
            jnp.concatenate(blocks, axis=1),
            jnp.concatenate([rot(b) for b in blocks], axis=1),
        ], axis=0)
        wide = jnp.dot(tab_ref[table_idx], stacked, preferred_element_type=jnp.float32)
        return [wide[:, g * lanes:(g + 1) * lanes] for g in range(len(blocks))]

    def scatter_y(a, middle):
        for hi in range(extent):
            y_ref[hi, a] = middle[hi * extent:(hi + 1) * extent]

    def stage_one(a0, blocks):
        for g, m in enumerate(apply(0, blocks)):
            scatter_y(a0 + g, m.astype(jnp.bfloat16))

    def write_out(a, value):
        for quarter in range(4):
            out_ref[(a % half_axis) * 4 + quarter, 0, a // half_axis] = value[quarter * rows:(quarter + 1) * rows]

    def recorded(v):
        wide = v.astype(jnp.float32)
        return wide == wide

    def magnitude(c):
        return jnp.sqrt(c * c + pltpu.roll(c, half, 1) ** 2)

    def init_group(i, carry):
        a0 = group * i
        initial = []
        for g in range(group):
            observed = obs_ref[0, a0 + g]
            value = jnp.where(recorded(observed), observed, jnp.zeros_like(observed))
            write_out(a0 + g, value)
            initial.append(value)
        stage_one(a0, initial)
        return carry

    lax.fori_loop(0, groups, init_group, 0, unroll=groups)

    def coeff_group(i):
        hi0 = group * i
        return apply(2, [y_ref[hi0 + g].reshape(plane, lanes) for g in range(group)])

    def init_hi(i, running):
        for coeffs in coeff_group(i):
            running = jnp.maximum(running, jnp.max(magnitude(coeffs), axis=0, keepdims=True))
        return running

    largest = lax.fori_loop(0, groups, init_hi, jnp.zeros((1, lanes), jnp.float32), unroll=groups)

    def sweep_step(k, carry):
        cutoff = largest * scales_ref[k]

        def thin_group(i, c2):
            thinned = []
            for coeffs in coeff_group(i):
                size_now = magnitude(coeffs)
                factor = jnp.maximum(size_now - cutoff, 0.0) / (jnp.maximum(size_now, cutoff) + 1e-06)
                thinned.append((coeffs * factor).astype(jnp.bfloat16))
            hi0 = group * i
            for g, back_mid in enumerate(apply(3, thinned)):
                back_mid = back_mid.astype(jnp.bfloat16)
                for a in range(extent):
                    v_ref[a, hi0 + g] = back_mid[a * extent:(a + 1) * extent]
            return c2

        lax.fori_loop(0, groups, thin_group, 0, unroll=groups)

        def back_group(i, c2):
            a0 = group * i
            returned = apply(1, [v_ref[a0 + g].reshape(plane, lanes) for g in range(group)])
            updated = []
            for g in range(group):
                observed = obs_ref[0, a0 + g].astype(jnp.float32)
                value = jnp.where(observed == observed, observed, returned[g]).astype(jnp.bfloat16)
                write_out(a0 + g, value)
                updated.append(value)

            @pl.when(k + 1 < sweeps)
            def _():
                stage_one(a0, updated)

            return c2

        lax.fori_loop(0, groups, back_group, 0, unroll=groups)
        return carry

    lax.fori_loop(0, sweeps, sweep_step, 0)


def run_patches(observed, sweeps, scales, tables):
    count, extent, plane, lanes = observed.shape
    block = pl.BlockSpec((1, extent, plane, lanes), lambda p, c, s: (p, 0, 0, 0))
    dests = extent // 2 * 4
    out_block = pl.BlockSpec((dests, 1, 2, plane // 4, lanes), lambda p, c, s: (0, p, 0, 0, 0))
    grid_spec = pltpu.PrefetchScalarGridSpec(
        num_scalar_prefetch=2,
        grid=(count,),
        in_specs=[block, pl.BlockSpec(tables.shape, lambda p, c, s: (0, 0, 0))],
        out_specs=out_block,
        scratch_shapes=[
            pltpu.VMEM((extent, extent, extent, lanes), jnp.bfloat16),
            pltpu.VMEM((extent, extent, extent, lanes), jnp.bfloat16),
        ],
    )
    return pl.pallas_call(
        pocs_kernel,
        grid_spec=grid_spec,
        out_shape=jax.ShapeDtypeStruct((dests, count, 2, plane // 4, lanes), jnp.bfloat16),
        compiler_params=pltpu.CompilerParams(dimension_semantics=("arbitrary",)),
    )(sweeps, scales, observed, tables)


def shards(spectra, sampled_mask, counts):
    extent = sampled_mask.shape[2]
    plane = extent * extent
    lane_count = spectra.shape[3]
    halfway = extent // 2
    regrouped = lax.all_to_all(spectra, "shot", split_axis=1, concat_axis=2, tiled=True)
    owned_count = regrouped.shape[1]
    observed = regrouped.reshape(owned_count, extent, plane, lane_count)
    marked = jnp.where(sampled_mask[0][..., None] > 0, observed, jnp.nan).astype(observed.dtype)
    tables = kernel_tables(extent)
    steps = jnp.arange(8, dtype=jnp.float32)
    scales = 0.5 * jnp.power(jnp.float32(0.6), steps)

    result = run_patches(marked, counts[0], scales, tables)
    dests = result.shape[0]
    top = result[:, :, 1]
    arrived = passed_along(top[:, -1], "shot", 1)
    earlier = jnp.concatenate([arrived[:, None], top[:, :-1]], axis=1).astype(jnp.float32)
    h = (jnp.arange(dests, dtype=jnp.int32) // (dests // halfway)).astype(jnp.float32)
    weight = ((h + 0.5) / halfway)[:, None, None, None]
    mixed = weight * result[:, :, 0].astype(jnp.float32) + (1.0 - weight) * earlier
    mixed = mixed.astype(jnp.bfloat16)
    return lax.all_to_all(mixed, "shot", split_axis=0, concat_axis=1, tiled=True)


def solution(mesh):
    return jax.shard_map(
        shards,
        mesh=mesh,
        in_specs=(P("az", None, "shot", None), P("az", "shot", None, None), P("az", "shot")),
        out_specs=P("az", None, "shot", None),
        check_vma=False,
    )
```

```python
import jax
import jax.numpy as jnp
from jax import lax
from jax.experimental import pallas as pl
from jax.experimental.pallas import tpu as pltpu
from jax.sharding import PartitionSpec as P


def passed_along(block, axis, distance):
    devices = range(lax.axis_size(axis))
    route = [(i - distance, i) for i in devices if i - distance in devices]
    return lax.ppermute(block, axis, route)


def dft_tables(extent):
    indices = jnp.arange(extent, dtype=jnp.int32)
    product = indices[:, None] * indices[None, :] % extent
    phase = product.astype(jnp.float32) * (2.0 * jnp.pi / extent)
    scale = extent ** (-0.5)
    cos_table = jnp.cos(phase) * scale
    sin_table = -jnp.sin(phase) * scale
    kron_real = jnp.kron(cos_table, cos_table) - jnp.kron(sin_table, sin_table)
    kron_imag = jnp.kron(cos_table, sin_table) + jnp.kron(sin_table, cos_table)
    return (
        cos_table.astype(jnp.bfloat16),
        sin_table.astype(jnp.bfloat16),
        kron_real.astype(jnp.bfloat16),
        kron_imag.astype(jnp.bfloat16),
    )


def kernel_tables(extent):
    cos_table, sin_table, kron_real, kron_imag = dft_tables(extent)
    eye = jnp.eye(extent, dtype=jnp.float32)

    def spread(table):
        return jnp.kron(table.astype(jnp.float32), eye).astype(jnp.bfloat16)

    return jnp.stack([
        jnp.concatenate([kron_real, kron_imag], axis=1),
        jnp.concatenate([kron_real, -kron_imag], axis=1),
        jnp.concatenate([spread(cos_table), spread(sin_table)], axis=1),
        jnp.concatenate([spread(cos_table), spread(-sin_table)], axis=1),
    ])


GROUP = 16


def pocs_kernel(counts_ref, scales_ref, obs_ref, tab_ref, out_ref, y_ref, v_ref):
    p = pl.program_id(0)
    extent = obs_ref.shape[1]
    lanes = obs_ref.shape[3]
    half = lanes // 2
    plane = obs_ref.shape[2]
    half_axis = extent // 2
    rows = plane // 4
    group = GROUP
    groups = extent // group
    sweeps = counts_ref[p]
    lower = lax.broadcasted_iota(jnp.int32, (1, lanes), 1) < half

    def rot(block):
        rolled = pltpu.roll(block, half, 1)
        return jnp.where(lower, -rolled, rolled)

    def apply(table_idx, blocks):
        stacked = jnp.concatenate([
            jnp.concatenate(blocks, axis=1),
            jnp.concatenate([rot(b) for b in blocks], axis=1),
        ], axis=0)
        wide = jnp.dot(tab_ref[table_idx], stacked, preferred_element_type=jnp.float32)
        return [wide[:, g * lanes:(g + 1) * lanes] for g in range(len(blocks))]

    def scatter_y(a, middle):
        for hi in range(extent):
            y_ref[hi, a] = middle[hi * extent:(hi + 1) * extent]

    def stage_one(a0, blocks):
        for g, m in enumerate(apply(0, blocks)):
            scatter_y(a0 + g, m.astype(jnp.bfloat16))

    def write_out(a, value):
        for quarter in range(4):
            out_ref[(a % half_axis) * 4 + quarter, 0, a // half_axis] = value[quarter * rows:(quarter + 1) * rows]

    def recorded(v):
        wide = v.astype(jnp.float32)
        return wide == wide

    def magnitude(c):
        return jnp.sqrt(c * c + pltpu.roll(c, half, 1) ** 2)

    def init_group(i, carry):
        a0 = group * i
        initial = []
        for g in range(group):
            observed = obs_ref[0, a0 + g]
            value = jnp.where(recorded(observed), observed, jnp.zeros_like(observed))
            write_out(a0 + g, value)
            initial.append(value)
        stage_one(a0, initial)
        return carry

    lax.fori_loop(0, groups, init_group, 0, unroll=groups)

    def coeff_group(i):
        hi0 = group * i
        return apply(2, [y_ref[hi0 + g].reshape(plane, lanes) for g in range(group)])

    def init_hi(i, running):
        for coeffs in coeff_group(i):
            running = jnp.maximum(running, jnp.max(magnitude(coeffs), axis=0, keepdims=True))
        return running

    largest = lax.fori_loop(0, groups, init_hi, jnp.zeros((1, lanes), jnp.float32), unroll=groups)

    def sweep_step(k, carry):
        cutoff = largest * scales_ref[k]

        def thin_group(i, c2):
            thinned = []
            for coeffs in coeff_group(i):
                size_now = magnitude(coeffs)
                factor = jnp.maximum(size_now - cutoff, 0.0) / (jnp.maximum(size_now, cutoff) + 1e-06)
                thinned.append((coeffs * factor).astype(jnp.bfloat16))
            hi0 = group * i
            for g, back_mid in enumerate(apply(3, thinned)):
                back_mid = back_mid.astype(jnp.bfloat16)
                for a in range(extent):
                    v_ref[a, hi0 + g] = back_mid[a * extent:(a + 1) * extent]
            return c2

        lax.fori_loop(0, groups, thin_group, 0, unroll=groups)

        def back_group(i, c2):
            a0 = group * i
            returned = apply(1, [v_ref[a0 + g].reshape(plane, lanes) for g in range(group)])
            updated = []
            for g in range(group):
                observed = obs_ref[0, a0 + g].astype(jnp.float32)
                value = jnp.where(observed == observed, observed, returned[g]).astype(jnp.bfloat16)
                write_out(a0 + g, value)
                updated.append(value)

            @pl.when(k + 1 < sweeps)
            def _():
                stage_one(a0, updated)

            return c2

        lax.fori_loop(0, groups, back_group, 0, unroll=groups)
        return carry

    lax.fori_loop(0, sweeps, sweep_step, 0)


def run_patches(observed, sweeps, scales, tables):
    count, extent, plane, lanes = observed.shape
    block = pl.BlockSpec((1, extent, plane, lanes), lambda p, c, s: (p, 0, 0, 0))
    dests = extent // 2 * 4
    out_block = pl.BlockSpec((dests, 1, 2, plane // 4, lanes), lambda p, c, s: (0, p, 0, 0, 0))
    grid_spec = pltpu.PrefetchScalarGridSpec(
        num_scalar_prefetch=2,
        grid=(count,),
        in_specs=[block, pl.BlockSpec(tables.shape, lambda p, c, s: (0, 0, 0))],
        out_specs=out_block,
        scratch_shapes=[
            pltpu.VMEM((extent, extent, extent, lanes), jnp.bfloat16),
            pltpu.VMEM((extent, extent, extent, lanes), jnp.bfloat16),
        ],
    )
    return pl.pallas_call(
        pocs_kernel,
        grid_spec=grid_spec,
        out_shape=jax.ShapeDtypeStruct((dests, count, 2, plane // 4, lanes), jnp.bfloat16),
        compiler_params=pltpu.CompilerParams(dimension_semantics=("arbitrary",)),
    )(sweeps, scales, observed, tables)


def shards(spectra, sampled_mask, counts):
    extent = sampled_mask.shape[2]
    plane = extent * extent
    lane_count = spectra.shape[3]
    halfway = extent // 2
    owned_count = counts.shape[1]
    tables = kernel_tables(extent)
    steps = jnp.arange(8, dtype=jnp.float32)
    scales = 0.5 * jnp.power(jnp.float32(0.6), steps)

    results = []
    for slot in range(owned_count):
        regrouped = lax.all_to_all(spectra[:, slot::owned_count], "shot", split_axis=1, concat_axis=2, tiled=True)
        observed = regrouped.reshape(1, extent, plane, lane_count)
        marked = jnp.where(sampled_mask[0, slot][None, ..., None] > 0, observed, jnp.nan).astype(observed.dtype)
        results.append(run_patches(marked, counts[0, slot:slot + 1], scales, tables)[:, 0])

    dests = results[0].shape[0]
    h = (jnp.arange(dests, dtype=jnp.int32) // (dests // halfway)).astype(jnp.float32)
    weight = ((h + 0.5) / halfway)[:, None, None]

    def blended(slot, earlier):
        mixed = weight * results[slot][:, 0].astype(jnp.float32) + (1.0 - weight) * earlier.astype(jnp.float32)
        mixed = mixed.astype(jnp.bfloat16)[:, None]
        return lax.all_to_all(mixed, "shot", split_axis=0, concat_axis=1, tiled=True)

    returned = [None] * owned_count
    for slot in range(1, owned_count):
        returned[slot] = blended(slot, results[slot - 1][:, 1])
    arrived = passed_along(results[-1][:, 1], "shot", 1)
    returned[0] = blended(0, arrived)
    stacked = jnp.stack(returned, axis=2)
    return stacked.reshape(1, -1, plane // 4, lane_count)


def solution(mesh):
    return jax.shard_map(
        shards,
        mesh=mesh,
        in_specs=(P("az", None, "shot", None), P("az", "shot", None, None), P("az", "shot")),
        out_specs=P("az", None, "shot", None),
        check_vma=False,
    )
```

```python
import jax
import jax.numpy as jnp
from jax import lax
from jax.experimental import pallas as pl
from jax.experimental.pallas import tpu as pltpu
from jax.sharding import PartitionSpec as P


def passed_along(block, axis, distance):
    devices = range(lax.axis_size(axis))
    route = [(i - distance, i) for i in devices if i - distance in devices]
    return lax.ppermute(block, axis, route)


def dft_tables(extent):
    indices = jnp.arange(extent, dtype=jnp.int32)
    product = indices[:, None] * indices[None, :] % extent
    phase = product.astype(jnp.float32) * (2.0 * jnp.pi / extent)
    scale = extent ** (-0.5)
    cos_table = jnp.cos(phase) * scale
    sin_table = -jnp.sin(phase) * scale
    kron_real = jnp.kron(cos_table, cos_table) - jnp.kron(sin_table, sin_table)
    kron_imag = jnp.kron(cos_table, sin_table) + jnp.kron(sin_table, cos_table)
    return (
        cos_table.astype(jnp.bfloat16),
        sin_table.astype(jnp.bfloat16),
        kron_real.astype(jnp.bfloat16),
        kron_imag.astype(jnp.bfloat16),
    )


def kernel_tables(extent):
    cos_table, sin_table, kron_real, kron_imag = dft_tables(extent)
    eye = jnp.eye(extent, dtype=jnp.float32)

    def spread(table):
        return jnp.kron(table.astype(jnp.float32), eye).astype(jnp.bfloat16)

    return jnp.stack([
        jnp.concatenate([kron_real, kron_imag], axis=1),
        jnp.concatenate([kron_real, -kron_imag], axis=1),
        jnp.concatenate([spread(cos_table), spread(sin_table)], axis=1),
        jnp.concatenate([spread(cos_table), spread(-sin_table)], axis=1),
    ])


GROUP = 16


def pocs_kernel(counts_ref, scales_ref, obs_ref, mask_ref, tab_ref, out_ref, y_ref, v_ref):
    p = pl.program_id(0)
    extent = obs_ref.shape[1]
    lanes = obs_ref.shape[3]
    half = lanes // 2
    plane = obs_ref.shape[2]
    half_axis = extent // 2
    rows = plane // 4
    group = GROUP
    groups = extent // group
    sweeps = counts_ref[p]
    lower = lax.broadcasted_iota(jnp.int32, (1, lanes), 1) < half

    def rot(block):
        rolled = pltpu.roll(block, half, 1)
        return jnp.where(lower, -rolled, rolled)

    def apply(table_idx, blocks):
        stacked = jnp.concatenate([
            jnp.concatenate(blocks, axis=1),
            jnp.concatenate([rot(b) for b in blocks], axis=1),
        ], axis=0)
        wide = jnp.dot(tab_ref[table_idx], stacked, preferred_element_type=jnp.float32)
        return [wide[:, g * lanes:(g + 1) * lanes] for g in range(len(blocks))]

    def scatter_y(a, middle):
        for hi in range(extent):
            y_ref[hi, a] = middle[hi * extent:(hi + 1) * extent]

    def stage_one(a0, blocks):
        for g, m in enumerate(apply(0, blocks)):
            scatter_y(a0 + g, m.astype(jnp.bfloat16))

    def write_out(a, value):
        for quarter in range(4):
            out_ref[(a % half_axis) * 4 + quarter, 0, a // half_axis] = value[quarter * rows:(quarter + 1) * rows]

    def magnitude(c):
        return jnp.sqrt(c * c + pltpu.roll(c, half, 1) ** 2)

    def init_group(i, carry):
        a0 = group * i
        initial = []
        for g in range(group):
            observed = obs_ref[0, a0 + g]
            value = jnp.where(mask_ref[0, a0 + g] > 0, observed, jnp.zeros_like(observed))
            write_out(a0 + g, value)
            initial.append(value)
        stage_one(a0, initial)
        return carry

    lax.fori_loop(0, groups, init_group, 0, unroll=groups)

    def coeff_group(i):
        hi0 = group * i
        return apply(2, [y_ref[hi0 + g].reshape(plane, lanes) for g in range(group)])

    def init_hi(i, running):
        for coeffs in coeff_group(i):
            running = jnp.maximum(running, jnp.max(magnitude(coeffs), axis=0, keepdims=True))
        return running

    largest = lax.fori_loop(0, groups, init_hi, jnp.zeros((1, lanes), jnp.float32), unroll=groups)

    def sweep_step(k, carry):
        cutoff = largest * scales_ref[k]

        def thin_group(i, c2):
            thinned = []
            for coeffs in coeff_group(i):
                size_now = magnitude(coeffs)
                factor = jnp.maximum(size_now - cutoff, 0.0) / (jnp.maximum(size_now, cutoff) + 1e-06)
                thinned.append((coeffs * factor).astype(jnp.bfloat16))
            hi0 = group * i
            for g, back_mid in enumerate(apply(3, thinned)):
                back_mid = back_mid.astype(jnp.bfloat16)
                for a in range(extent):
                    v_ref[a, hi0 + g] = back_mid[a * extent:(a + 1) * extent]
            return c2

        lax.fori_loop(0, groups, thin_group, 0, unroll=groups)

        def back_group(i, c2):
            a0 = group * i
            returned = apply(1, [v_ref[a0 + g].reshape(plane, lanes) for g in range(group)])
            updated = []
            for g in range(group):
                observed = obs_ref[0, a0 + g].astype(jnp.float32)
                value = jnp.where(mask_ref[0, a0 + g] > 0, observed, returned[g]).astype(jnp.bfloat16)
                write_out(a0 + g, value)
                updated.append(value)

            @pl.when(k + 1 < sweeps)
            def _():
                stage_one(a0, updated)

            return c2

        lax.fori_loop(0, groups, back_group, 0, unroll=groups)
        return carry

    lax.fori_loop(0, sweeps, sweep_step, 0)


def run_patches(observed, maskb, sweeps, scales, tables):
    count, extent, plane, lanes = observed.shape
    block = pl.BlockSpec((1, extent, plane, lanes), lambda p, c, s: (p, 0, 0, 0))
    dests = extent // 2 * 4
    out_block = pl.BlockSpec((dests, 1, 2, plane // 4, lanes), lambda p, c, s: (0, p, 0, 0, 0))
    grid_spec = pltpu.PrefetchScalarGridSpec(
        num_scalar_prefetch=2,
        grid=(count,),
        in_specs=[block, block, pl.BlockSpec(tables.shape, lambda p, c, s: (0, 0, 0))],
        out_specs=out_block,
        scratch_shapes=[
            pltpu.VMEM((extent, extent, extent, lanes), jnp.bfloat16),
            pltpu.VMEM((extent, extent, extent, lanes), jnp.bfloat16),
        ],
    )
    return pl.pallas_call(
        pocs_kernel,
        grid_spec=grid_spec,
        out_shape=jax.ShapeDtypeStruct((dests, count, 2, plane // 4, lanes), jnp.bfloat16),
        compiler_params=pltpu.CompilerParams(dimension_semantics=("arbitrary",)),
    )(sweeps, scales, observed, maskb, tables)


def shards(spectra, sampled_mask, counts):
    extent = sampled_mask.shape[2]
    plane = extent * extent
    lane_count = spectra.shape[3]
    halfway = extent // 2
    devices = lax.axis_size("shot")
    owned_count = counts.shape[1]
    chunk = owned_count // 2
    tables = kernel_tables(extent)
    steps = jnp.arange(8, dtype=jnp.float32)
    scales = 0.5 * jnp.power(jnp.float32(0.6), steps)
    by_owner = spectra.reshape((1, devices, owned_count) + spectra.shape[2:])

    pieces = []
    for first in range(0, owned_count, chunk):
        part = by_owner[:, :, first:first + chunk].reshape((1, devices * chunk) + spectra.shape[2:])
        regrouped = lax.all_to_all(part, "shot", split_axis=1, concat_axis=2, tiled=True)
        observed = regrouped.reshape(chunk, extent, plane, lane_count)
        recorded = (sampled_mask[0, first:first + chunk] > 0).astype(jnp.bfloat16)
        maskb = jnp.broadcast_to(recorded[..., None], observed.shape)
        pieces.append(run_patches(observed, maskb, counts[0, first:first + chunk], scales, tables))
    result = jnp.concatenate(pieces, axis=1)
    dests = result.shape[0]
    top = result[:, :, 1]
    arrived = passed_along(top[:, -1], "shot", 1)
    earlier = jnp.concatenate([arrived[:, None], top[:, :-1]], axis=1).astype(jnp.float32)
    h = (jnp.arange(dests, dtype=jnp.int32) // (dests // halfway)).astype(jnp.float32)
    weight = ((h + 0.5) / halfway)[:, None, None, None]
    mixed = weight * result[:, :, 0].astype(jnp.float32) + (1.0 - weight) * earlier
    mixed = mixed.astype(jnp.bfloat16)
    return lax.all_to_all(mixed, "shot", split_axis=0, concat_axis=1, tiled=True)


def solution(mesh):
    return jax.shard_map(
        shards,
        mesh=mesh,
        in_specs=(P("az", None, "shot", None), P("az", "shot", None, None), P("az", "shot")),
        out_specs=P("az", None, "shot", None),
        check_vma=False,
    )
```

```python
import ml_dtypes
import numpy as np

import jax
import jax.numpy as jnp
from jax import lax
from jax.experimental import pallas as pl
from jax.experimental.pallas import tpu as pltpu
from jax.sharding import PartitionSpec as P


def passed_along(block, axis, distance):
    devices = range(lax.axis_size(axis))
    route = [(i - distance, i) for i in devices if i - distance in devices]
    return lax.ppermute(block, axis, route)


def kernel_tables(extent):
    indices = np.arange(extent, dtype=np.int32)
    product = indices[:, None] * indices[None, :] % extent
    phase = product.astype(np.float32) * np.float32(2.0 * np.pi / extent)
    scale = np.float32(extent ** (-0.5))
    cos_table = np.cos(phase) * scale
    sin_table = -np.sin(phase) * scale
    kron_real = np.kron(cos_table, cos_table) - np.kron(sin_table, sin_table)
    kron_imag = np.kron(cos_table, sin_table) + np.kron(sin_table, cos_table)
    bf16 = ml_dtypes.bfloat16
    cos_b, sin_b = cos_table.astype(bf16), sin_table.astype(bf16)
    real_b, imag_b = kron_real.astype(bf16), kron_imag.astype(bf16)
    eye = np.eye(extent, dtype=np.float32)

    def spread(table):
        return np.kron(table.astype(np.float32), eye).astype(bf16)

    return jnp.asarray(np.stack([
        np.concatenate([real_b, imag_b], axis=1),
        np.concatenate([real_b, -imag_b], axis=1),
        np.concatenate([spread(cos_b), spread(sin_b)], axis=1),
        np.concatenate([spread(cos_b), spread(-sin_b)], axis=1),
    ]))


GROUP = 16


def pocs_kernel(counts_ref, scales_ref, obs_ref, mask_ref, tab_ref, out_ref, y_ref, v_ref):
    p = pl.program_id(0)
    extent = obs_ref.shape[1]
    lanes = obs_ref.shape[3]
    half = lanes // 2
    plane = obs_ref.shape[2]
    half_axis = extent // 2
    rows = plane // 4
    group = GROUP
    groups = extent // group
    sweeps = counts_ref[p]
    lower = lax.broadcasted_iota(jnp.int32, (1, lanes), 1) < half

    def rot(block):
        rolled = pltpu.roll(block, half, 1)
        return jnp.where(lower, -rolled, rolled)

    def apply(table_idx, blocks):
        stacked = jnp.concatenate([
            jnp.concatenate(blocks, axis=1),
            jnp.concatenate([rot(b) for b in blocks], axis=1),
        ], axis=0)
        wide = jnp.dot(tab_ref[table_idx], stacked, preferred_element_type=jnp.float32)
        return [wide[:, g * lanes:(g + 1) * lanes] for g in range(len(blocks))]

    def scatter_y(a, middle):
        for hi in range(extent):
            y_ref[hi, a] = middle[hi * extent:(hi + 1) * extent]

    def stage_one(a0, blocks):
        for g, m in enumerate(apply(0, blocks)):
            scatter_y(a0 + g, m.astype(jnp.bfloat16))

    def write_out(a, value):
        for quarter in range(4):
            out_ref[(a % half_axis) * 4 + quarter, 0, a // half_axis] = value[quarter * rows:(quarter + 1) * rows]

    def magnitude(c):
        return jnp.sqrt(c * c + pltpu.roll(c, half, 1) ** 2)

    def init_group(i, carry):
        a0 = group * i
        initial = []
        for g in range(group):
            observed = obs_ref[0, a0 + g]
            value = jnp.where(mask_ref[0, a0 + g] > 0, observed, jnp.zeros_like(observed))
            write_out(a0 + g, value)
            initial.append(value)
        stage_one(a0, initial)
        return carry

    lax.fori_loop(0, groups, init_group, 0, unroll=groups)

    def coeff_group(i):
        hi0 = group * i
        return apply(2, [y_ref[hi0 + g].reshape(plane, lanes) for g in range(group)])

    def init_hi(i, running):
        for coeffs in coeff_group(i):
            running = jnp.maximum(running, jnp.max(magnitude(coeffs), axis=0, keepdims=True))
        return running

    largest = lax.fori_loop(0, groups, init_hi, jnp.zeros((1, lanes), jnp.float32), unroll=groups)

    def sweep_step(k, carry):
        cutoff = largest * scales_ref[k]

        def thin_group(i, c2):
            thinned = []
            for coeffs in coeff_group(i):
                size_now = magnitude(coeffs)
                factor = jnp.maximum(size_now - cutoff, 0.0) / (jnp.maximum(size_now, cutoff) + 1e-06)
                thinned.append((coeffs * factor).astype(jnp.bfloat16))
            hi0 = group * i
            for g, back_mid in enumerate(apply(3, thinned)):
                back_mid = back_mid.astype(jnp.bfloat16)
                for a in range(extent):
                    v_ref[a, hi0 + g] = back_mid[a * extent:(a + 1) * extent]
            return c2

        lax.fori_loop(0, groups, thin_group, 0, unroll=groups)

        def back_group(i, c2):
            a0 = group * i
            returned = apply(1, [v_ref[a0 + g].reshape(plane, lanes) for g in range(group)])
            updated = []
            for g in range(group):
                observed = obs_ref[0, a0 + g].astype(jnp.float32)
                value = jnp.where(mask_ref[0, a0 + g] > 0, observed, returned[g]).astype(jnp.bfloat16)
                write_out(a0 + g, value)
                updated.append(value)

            @pl.when(k + 1 < sweeps)
            def _():
                stage_one(a0, updated)

            return c2

        lax.fori_loop(0, groups, back_group, 0, unroll=groups)
        return carry

    lax.fori_loop(0, sweeps, sweep_step, 0)


def run_patches(observed, maskb, sweeps, scales, tables):
    count, extent, plane, lanes = observed.shape
    block = pl.BlockSpec((1, extent, plane, lanes), lambda p, c, s: (p, 0, 0, 0))
    dests = extent // 2 * 4
    out_block = pl.BlockSpec((dests, 1, 2, plane // 4, lanes), lambda p, c, s: (0, p, 0, 0, 0))
    grid_spec = pltpu.PrefetchScalarGridSpec(
        num_scalar_prefetch=2,
        grid=(count,),
        in_specs=[block, block, pl.BlockSpec(tables.shape, lambda p, c, s: (0, 0, 0))],
        out_specs=out_block,
        scratch_shapes=[
            pltpu.VMEM((extent, extent, extent, lanes), jnp.bfloat16),
            pltpu.VMEM((extent, extent, extent, lanes), jnp.bfloat16),
        ],
    )
    return pl.pallas_call(
        pocs_kernel,
        grid_spec=grid_spec,
        out_shape=jax.ShapeDtypeStruct((dests, count, 2, plane // 4, lanes), jnp.bfloat16),
        compiler_params=pltpu.CompilerParams(dimension_semantics=("arbitrary",)),
    )(sweeps, scales, observed, maskb, tables)


def shards(spectra, sampled_mask, counts):
    extent = sampled_mask.shape[2]
    plane = extent * extent
    lane_count = spectra.shape[3]
    halfway = extent // 2
    devices = lax.axis_size("shot")
    owned_count = counts.shape[1]
    chunk = owned_count // 2
    tables = kernel_tables(extent)
    steps = jnp.arange(8, dtype=jnp.float32)
    scales = 0.5 * jnp.power(jnp.float32(0.6), steps)
    by_owner = spectra.reshape((1, devices, owned_count) + spectra.shape[2:])

    pieces = []
    for first in range(0, owned_count, chunk):
        part = by_owner[:, :, first:first + chunk].reshape((1, devices * chunk) + spectra.shape[2:])
        regrouped = lax.all_to_all(part, "shot", split_axis=1, concat_axis=2, tiled=True)
        observed = regrouped.reshape(chunk, extent, plane, lane_count)
        recorded = (sampled_mask[0, first:first + chunk] > 0).astype(jnp.bfloat16)
        maskb = jnp.broadcast_to(recorded[..., None], observed.shape)
        pieces.append(run_patches(observed, maskb, counts[0, first:first + chunk], scales, tables))
    result = jnp.concatenate(pieces, axis=1)
    dests = result.shape[0]
    top = result[:, :, 1]
    arrived = passed_along(top[:, -1], "shot", 1)
    earlier = jnp.concatenate([arrived[:, None], top[:, :-1]], axis=1).astype(jnp.float32)
    h = (jnp.arange(dests, dtype=jnp.int32) // (dests // halfway)).astype(jnp.float32)
    weight = ((h + 0.5) / halfway)[:, None, None, None]
    mixed = weight * result[:, :, 0].astype(jnp.float32) + (1.0 - weight) * earlier
    mixed = mixed.astype(jnp.bfloat16)
    return lax.all_to_all(mixed, "shot", split_axis=0, concat_axis=1, tiled=True)


def solution(mesh):
    return jax.shard_map(
        shards,
        mesh=mesh,
        in_specs=(P("az", None, "shot", None), P("az", "shot", None, None), P("az", "shot")),
        out_specs=P("az", None, "shot", None),
        check_vma=False,
    )
```

```python
import ml_dtypes
import numpy as np

import jax
import jax.numpy as jnp
from jax import lax
from jax.experimental import pallas as pl
from jax.experimental.pallas import tpu as pltpu
from jax.sharding import PartitionSpec as P


def passed_along(block, axis, distance):
    devices = range(lax.axis_size(axis))
    route = [(i - distance, i) for i in devices if i - distance in devices]
    return lax.ppermute(block, axis, route)


def kernel_tables(extent):
    indices = np.arange(extent, dtype=np.int32)
    product = indices[:, None] * indices[None, :] % extent
    phase = product.astype(np.float32) * np.float32(2.0 * np.pi / extent)
    scale = np.float32(extent ** (-0.5))
    cos_table = np.cos(phase) * scale
    sin_table = -np.sin(phase) * scale
    kron_real = np.kron(cos_table, cos_table) - np.kron(sin_table, sin_table)
    kron_imag = np.kron(cos_table, sin_table) + np.kron(sin_table, cos_table)
    bf16 = ml_dtypes.bfloat16
    cos_b, sin_b = cos_table.astype(bf16), sin_table.astype(bf16)
    real_b, imag_b = kron_real.astype(bf16), kron_imag.astype(bf16)
    eye = np.eye(extent, dtype=np.float32)

    def spread(table):
        return np.kron(table.astype(np.float32), eye).astype(bf16)

    return jnp.asarray(np.stack([
        np.concatenate([real_b, imag_b], axis=1),
        np.concatenate([real_b, -imag_b], axis=1),
        np.concatenate([spread(cos_b), spread(sin_b)], axis=1),
        np.concatenate([spread(cos_b), spread(-sin_b)], axis=1),
    ]))


GROUP = 16


def pocs_kernel(counts_ref, scales_ref, obs_ref, mask_ref, tab_ref, out_ref, y_ref, v_ref):
    p = pl.program_id(0)
    extent = obs_ref.shape[1]
    lanes = obs_ref.shape[3]
    half = lanes // 2
    plane = obs_ref.shape[2]
    half_axis = extent // 2
    rows = plane // 4
    group = GROUP
    groups = extent // group
    sweeps = counts_ref[p]
    lower = lax.broadcasted_iota(jnp.int32, (1, lanes), 1) < half

    def rot(block):
        rolled = pltpu.roll(block, half, 1)
        return jnp.where(lower, -rolled, rolled)

    def apply(table_idx, blocks):
        stacked = jnp.concatenate([
            jnp.concatenate(blocks, axis=1),
            jnp.concatenate([rot(b) for b in blocks], axis=1),
        ], axis=0)
        wide = jnp.dot(tab_ref[table_idx], stacked, preferred_element_type=jnp.float32)
        return [wide[:, g * lanes:(g + 1) * lanes] for g in range(len(blocks))]

    def scatter_y(a, middle):
        for hi in range(extent):
            y_ref[hi, a] = middle[hi * extent:(hi + 1) * extent]

    def stage_one(a0, blocks):
        for g, m in enumerate(apply(0, blocks)):
            scatter_y(a0 + g, m.astype(jnp.bfloat16))

    def write_out(a, value):
        for quarter in range(4):
            out_ref[(a % half_axis) * 4 + quarter, 0, a // half_axis] = value[quarter * rows:(quarter + 1) * rows]

    def init_group(i, carry):
        a0 = group * i
        initial = []
        for g in range(group):
            observed = obs_ref[0, a0 + g]
            value = jnp.where(mask_ref[0, a0 + g] > 0, observed, jnp.zeros_like(observed))
            write_out(a0 + g, value)
            initial.append(value)
        stage_one(a0, initial)
        return carry

    lax.fori_loop(0, groups, init_group, 0, unroll=groups)

    def coeff_group(i):
        hi0 = group * i
        return apply(2, [y_ref[hi0 + g].reshape(plane, lanes) for g in range(group)])

    def init_hi(i, running):
        for coeffs in coeff_group(i):
            square = coeffs * coeffs
            running = jnp.maximum(running, jnp.max(square + pltpu.roll(square, half, 1), axis=0, keepdims=True))
        return running

    largest = jnp.sqrt(lax.fori_loop(0, groups, init_hi, jnp.zeros((1, lanes), jnp.float32), unroll=groups))

    def sweep_step(k, carry):
        cutoff = largest * scales_ref[k]

        def thin_group(i, c2):
            thinned = []
            blocks = coeff_group(i)
            for b in range(0, len(blocks), 2):
                first, second = blocks[b], blocks[b + 1]
                sq0 = first * first
                sq1 = second * second
                packed = jnp.where(lower, sq0 + pltpu.roll(sq0, half, 1), sq1 + pltpu.roll(sq1, half, 1))
                size_now = jnp.sqrt(packed)
                factor = jnp.maximum(size_now - cutoff, 0.0) / (jnp.maximum(size_now, cutoff) + 1e-06)
                swapped = pltpu.roll(factor, half, 1)
                thinned.append((first * jnp.where(lower, factor, swapped)).astype(jnp.bfloat16))
                thinned.append((second * jnp.where(lower, swapped, factor)).astype(jnp.bfloat16))
            hi0 = group * i
            for g, back_mid in enumerate(apply(3, thinned)):
                back_mid = back_mid.astype(jnp.bfloat16)
                for a in range(extent):
                    v_ref[a, hi0 + g] = back_mid[a * extent:(a + 1) * extent]
            return c2

        lax.fori_loop(0, groups, thin_group, 0, unroll=groups)

        def back_group(i, c2):
            a0 = group * i
            returned = apply(1, [v_ref[a0 + g].reshape(plane, lanes) for g in range(group)])
            updated = []
            for g in range(group):
                observed = obs_ref[0, a0 + g].astype(jnp.float32)
                value = jnp.where(mask_ref[0, a0 + g] > 0, observed, returned[g]).astype(jnp.bfloat16)
                write_out(a0 + g, value)
                updated.append(value)

            @pl.when(k + 1 < sweeps)
            def _():
                stage_one(a0, updated)

            return c2

        lax.fori_loop(0, groups, back_group, 0, unroll=groups)
        return carry

    lax.fori_loop(0, sweeps, sweep_step, 0)


def run_patches(observed, maskb, sweeps, scales, tables):
    count, extent, plane, lanes = observed.shape
    block = pl.BlockSpec((1, extent, plane, lanes), lambda p, c, s: (p, 0, 0, 0))
    dests = extent // 2 * 4
    out_block = pl.BlockSpec((dests, 1, 2, plane // 4, lanes), lambda p, c, s: (0, p, 0, 0, 0))
    grid_spec = pltpu.PrefetchScalarGridSpec(
        num_scalar_prefetch=2,
        grid=(count,),
        in_specs=[block, block, pl.BlockSpec(tables.shape, lambda p, c, s: (0, 0, 0))],
        out_specs=out_block,
        scratch_shapes=[
            pltpu.VMEM((extent, extent, extent, lanes), jnp.bfloat16),
            pltpu.VMEM((extent, extent, extent, lanes), jnp.bfloat16),
        ],
    )
    return pl.pallas_call(
        pocs_kernel,
        grid_spec=grid_spec,
        out_shape=jax.ShapeDtypeStruct((dests, count, 2, plane // 4, lanes), jnp.bfloat16),
        compiler_params=pltpu.CompilerParams(dimension_semantics=("arbitrary",)),
    )(sweeps, scales, observed, maskb, tables)


def shards(spectra, sampled_mask, counts):
    extent = sampled_mask.shape[2]
    plane = extent * extent
    lane_count = spectra.shape[3]
    halfway = extent // 2
    devices = lax.axis_size("shot")
    owned_count = counts.shape[1]
    chunk = owned_count // 2
    tables = kernel_tables(extent)
    steps = jnp.arange(8, dtype=jnp.float32)
    scales = 0.5 * jnp.power(jnp.float32(0.6), steps)
    by_owner = spectra.reshape((1, devices, owned_count) + spectra.shape[2:])

    pieces = []
    for first in range(0, owned_count, chunk):
        part = by_owner[:, :, first:first + chunk].reshape((1, devices * chunk) + spectra.shape[2:])
        regrouped = lax.all_to_all(part, "shot", split_axis=1, concat_axis=2, tiled=True)
        observed = regrouped.reshape(chunk, extent, plane, lane_count)
        recorded = (sampled_mask[0, first:first + chunk] > 0).astype(jnp.bfloat16)
        maskb = jnp.broadcast_to(recorded[..., None], observed.shape)
        pieces.append(run_patches(observed, maskb, counts[0, first:first + chunk], scales, tables))
    result = jnp.concatenate(pieces, axis=1)
    dests = result.shape[0]
    top = result[:, :, 1]
    arrived = passed_along(top[:, -1], "shot", 1)
    earlier = jnp.concatenate([arrived[:, None], top[:, :-1]], axis=1).astype(jnp.float32)
    h = (jnp.arange(dests, dtype=jnp.int32) // (dests // halfway)).astype(jnp.float32)
    weight = ((h + 0.5) / halfway)[:, None, None, None]
    mixed = weight * result[:, :, 0].astype(jnp.float32) + (1.0 - weight) * earlier
    mixed = mixed.astype(jnp.bfloat16)
    return lax.all_to_all(mixed, "shot", split_axis=0, concat_axis=1, tiled=True)


def solution(mesh):
    return jax.shard_map(
        shards,
        mesh=mesh,
        in_specs=(P("az", None, "shot", None), P("az", "shot", None, None), P("az", "shot")),
        out_specs=P("az", None, "shot", None),
        check_vma=False,
    )
```

```python
import ml_dtypes
import numpy as np

import jax
import jax.numpy as jnp
from jax import lax
from jax.experimental import pallas as pl
from jax.experimental.pallas import tpu as pltpu
from jax.sharding import PartitionSpec as P


def passed_along(block, axis, distance):
    devices = range(lax.axis_size(axis))
    route = [(i - distance, i) for i in devices if i - distance in devices]
    return lax.ppermute(block, axis, route)


def kernel_tables(extent):
    indices = np.arange(extent, dtype=np.int32)
    product = indices[:, None] * indices[None, :] % extent
    phase = product.astype(np.float32) * np.float32(2.0 * np.pi / extent)
    scale = np.float32(extent ** (-0.5))
    cos_table = np.cos(phase) * scale
    sin_table = -np.sin(phase) * scale
    kron_real = np.kron(cos_table, cos_table) - np.kron(sin_table, sin_table)
    kron_imag = np.kron(cos_table, sin_table) + np.kron(sin_table, cos_table)
    bf16 = ml_dtypes.bfloat16
    cos_b, sin_b = cos_table.astype(bf16), sin_table.astype(bf16)
    real_b, imag_b = kron_real.astype(bf16), kron_imag.astype(bf16)
    eye = np.eye(extent, dtype=np.float32)

    def spread(table):
        return np.kron(table.astype(np.float32), eye).astype(bf16)

    return jnp.asarray(np.stack([
        np.concatenate([real_b, imag_b], axis=1),
        np.concatenate([real_b, -imag_b], axis=1),
        np.concatenate([spread(cos_b), spread(sin_b)], axis=1),
        np.concatenate([spread(cos_b), spread(-sin_b)], axis=1),
    ]))


GROUP = 16


def pocs_kernel(counts_ref, scales_ref, obs_ref, mask_ref, tab_ref, out_ref, y_ref, v_ref, m_ref):
    p = pl.program_id(0)
    extent = obs_ref.shape[1]
    lanes = obs_ref.shape[3]
    half = lanes // 2
    plane = obs_ref.shape[2]
    half_axis = extent // 2
    rows = plane // 4
    group = GROUP
    groups = extent // group
    sweeps = counts_ref[p]
    lower = lax.broadcasted_iota(jnp.int32, (1, lanes), 1) < half
    columns = jnp.transpose(mask_ref[0].astype(jnp.float32))
    for a in range(extent):
        m_ref[a] = jnp.broadcast_to(columns[:, a:a + 1], (plane, lanes)).astype(jnp.bfloat16)

    def sampled(a):
        return m_ref[a] > 0

    def rot(block):
        rolled = pltpu.roll(block, half, 1)
        return jnp.where(lower, -rolled, rolled)

    def apply(table_idx, blocks):
        stacked = jnp.concatenate([
            jnp.concatenate(blocks, axis=1),
            jnp.concatenate([rot(b) for b in blocks], axis=1),
        ], axis=0)
        wide = jnp.dot(tab_ref[table_idx], stacked, preferred_element_type=jnp.float32)
        return [wide[:, g * lanes:(g + 1) * lanes] for g in range(len(blocks))]

    def scatter_y(a, middle):
        for hi in range(extent):
            y_ref[hi, a] = middle[hi * extent:(hi + 1) * extent]

    def stage_one(a0, blocks):
        for g, m in enumerate(apply(0, blocks)):
            scatter_y(a0 + g, m.astype(jnp.bfloat16))

    def write_out(a, value):
        for quarter in range(4):
            out_ref[(a % half_axis) * 4 + quarter, 0, a // half_axis] = value[quarter * rows:(quarter + 1) * rows]

    def init_group(i, carry):
        a0 = group * i
        initial = []
        for g in range(group):
            observed = obs_ref[0, a0 + g]
            value = jnp.where(sampled(a0 + g), observed, jnp.zeros_like(observed))
            write_out(a0 + g, value)
            initial.append(value)
        stage_one(a0, initial)
        return carry

    for i in range(groups):
        init_group(i, 0)

    def coeff_group(i):
        hi0 = group * i
        return apply(2, [y_ref[hi0 + g].reshape(plane, lanes) for g in range(group)])

    def init_hi(i, running):
        for coeffs in coeff_group(i):
            square = coeffs * coeffs
            running = jnp.maximum(running, jnp.max(square + pltpu.roll(square, half, 1), axis=0, keepdims=True))
        return running

    running = jnp.zeros((1, lanes), jnp.float32)
    for i in range(groups):
        running = init_hi(i, running)
    largest = jnp.sqrt(running)

    def sweep_step(k, carry):
        cutoff = largest * scales_ref[k]

        def thin_group(i, c2):
            thinned = []
            blocks = coeff_group(i)
            for b in range(0, len(blocks), 2):
                first, second = blocks[b], blocks[b + 1]
                sq0 = first * first
                sq1 = second * second
                packed = jnp.where(lower, sq0 + pltpu.roll(sq0, half, 1), sq1 + pltpu.roll(sq1, half, 1))
                size_now = jnp.sqrt(packed)
                factor = jnp.maximum(size_now - cutoff, 0.0) / (jnp.maximum(size_now, cutoff) + 1e-06)
                swapped = pltpu.roll(factor, half, 1)
                thinned.append((first * jnp.where(lower, factor, swapped)).astype(jnp.bfloat16))
                thinned.append((second * jnp.where(lower, swapped, factor)).astype(jnp.bfloat16))
            hi0 = group * i
            for g, back_mid in enumerate(apply(3, thinned)):
                back_mid = back_mid.astype(jnp.bfloat16)
                for a in range(extent):
                    v_ref[a, hi0 + g] = back_mid[a * extent:(a + 1) * extent]
            return c2

        for i in range(groups):
            thin_group(i, 0)

        def back_group(i, c2):
            a0 = group * i
            returned = apply(1, [v_ref[a0 + g].reshape(plane, lanes) for g in range(group)])
            updated = []
            for g in range(group):
                observed = obs_ref[0, a0 + g].astype(jnp.float32)
                value = jnp.where(sampled(a0 + g), observed, returned[g]).astype(jnp.bfloat16)
                write_out(a0 + g, value)
                updated.append(value)

            @pl.when(k + 1 < sweeps)
            def _():
                stage_one(a0, updated)

            return c2

        for i in range(groups):
            back_group(i, 0)
        return carry

    lax.fori_loop(0, sweeps, sweep_step, 0)


def run_patches(observed, maskb, sweeps, scales, tables):
    count, extent, plane, lanes = observed.shape
    block = pl.BlockSpec((1, extent, plane, lanes), lambda p, c, s: (p, 0, 0, 0))
    dests = extent // 2 * 4
    out_block = pl.BlockSpec((dests, 1, 2, plane // 4, lanes), lambda p, c, s: (0, p, 0, 0, 0))
    grid_spec = pltpu.PrefetchScalarGridSpec(
        num_scalar_prefetch=2,
        grid=(count,),
        in_specs=[block, pl.BlockSpec((1, extent, plane), lambda p, c, s: (p, 0, 0)), pl.BlockSpec(tables.shape, lambda p, c, s: (0, 0, 0))],
        out_specs=out_block,
        scratch_shapes=[
            pltpu.VMEM((extent, extent, extent, lanes), jnp.bfloat16),
            pltpu.VMEM((extent, extent, extent, lanes), jnp.bfloat16),
            pltpu.VMEM((extent, plane, lanes), jnp.bfloat16),
        ],
    )
    return pl.pallas_call(
        pocs_kernel,
        grid_spec=grid_spec,
        out_shape=jax.ShapeDtypeStruct((dests, count, 2, plane // 4, lanes), jnp.bfloat16),
        compiler_params=pltpu.CompilerParams(dimension_semantics=("arbitrary",)),
    )(sweeps, scales, observed, maskb, tables)


def shards(spectra, sampled_mask, counts):
    extent = sampled_mask.shape[2]
    plane = extent * extent
    lane_count = spectra.shape[3]
    halfway = extent // 2
    devices = lax.axis_size("shot")
    owned_count = counts.shape[1]
    chunk = owned_count // 2
    tables = kernel_tables(extent)
    steps = jnp.arange(8, dtype=jnp.float32)
    scales = 0.5 * jnp.power(jnp.float32(0.6), steps)
    by_owner = spectra.reshape((1, devices, owned_count) + spectra.shape[2:])

    pieces = []
    for first in range(0, owned_count, chunk):
        part = by_owner[:, :, first:first + chunk].reshape((1, devices * chunk) + spectra.shape[2:])
        regrouped = lax.all_to_all(part, "shot", split_axis=1, concat_axis=2, tiled=True)
        observed = regrouped.reshape(chunk, extent, plane, lane_count)
        maskb = sampled_mask[0, first:first + chunk]
        pieces.append(run_patches(observed, maskb, counts[0, first:first + chunk], scales, tables))
    result = jnp.concatenate(pieces, axis=1)
    dests = result.shape[0]
    top = result[:, :, 1]
    arrived = passed_along(top[:, -1], "shot", 1)
    earlier = jnp.concatenate([arrived[:, None], top[:, :-1]], axis=1).astype(jnp.float32)
    h = (jnp.arange(dests, dtype=jnp.int32) // (dests // halfway)).astype(jnp.float32)
    weight = ((h + 0.5) / halfway)[:, None, None, None]
    mixed = weight * result[:, :, 0].astype(jnp.float32) + (1.0 - weight) * earlier
    mixed = mixed.astype(jnp.bfloat16)
    return lax.all_to_all(mixed, "shot", split_axis=0, concat_axis=1, tiled=True)


def solution(mesh):
    return jax.shard_map(
        shards,
        mesh=mesh,
        in_specs=(P("az", None, "shot", None), P("az", "shot", None, None), P("az", "shot")),
        out_specs=P("az", None, "shot", None),
        check_vma=False,
    )
```

```python
import ml_dtypes
import numpy as np

import jax
import jax.numpy as jnp
from jax import lax
from jax.experimental import pallas as pl
from jax.experimental.pallas import tpu as pltpu
from jax.sharding import PartitionSpec as P


def passed_along(block, axis, distance):
    devices = range(lax.axis_size(axis))
    route = [(i - distance, i) for i in devices if i - distance in devices]
    return lax.ppermute(block, axis, route)


def kernel_tables(extent):
    indices = np.arange(extent, dtype=np.int32)
    product = indices[:, None] * indices[None, :] % extent
    phase = product.astype(np.float32) * np.float32(2.0 * np.pi / extent)
    scale = np.float32(extent ** (-0.5))
    cos_table = np.cos(phase) * scale
    sin_table = -np.sin(phase) * scale
    kron_real = np.kron(cos_table, cos_table) - np.kron(sin_table, sin_table)
    kron_imag = np.kron(cos_table, sin_table) + np.kron(sin_table, cos_table)
    bf16 = ml_dtypes.bfloat16
    cos_b, sin_b = cos_table.astype(bf16), sin_table.astype(bf16)
    real_b, imag_b = kron_real.astype(bf16), kron_imag.astype(bf16)
    eye = np.eye(extent, dtype=np.float32)

    def spread(table):
        return np.kron(table.astype(np.float32), eye).astype(bf16)

    return jnp.asarray(np.stack([
        np.concatenate([real_b, imag_b], axis=1),
        np.concatenate([real_b, -imag_b], axis=1),
        np.concatenate([spread(cos_b), spread(sin_b)], axis=1),
        np.concatenate([spread(cos_b), spread(-sin_b)], axis=1),
    ]))


GROUP = 16


def pocs_kernel(counts_ref, scales_ref, obs_ref, mask_ref, tab_ref, out_ref, y_ref, v_ref):
    p = pl.program_id(0)
    extent = mask_ref.shape[1]
    lanes = mask_ref.shape[3]
    half = lanes // 2
    plane = mask_ref.shape[2]
    sources = obs_ref.shape[0] // extent

    def obs(a):
        return obs_ref[pl.ds(a * sources, sources), 0].reshape(plane, lanes)

    half_axis = extent // 2
    rows = plane // 4
    group = GROUP
    groups = extent // group
    sweeps = counts_ref[p]
    lower = lax.broadcasted_iota(jnp.int32, (1, lanes), 1) < half

    def rot(block):
        rolled = pltpu.roll(block, half, 1)
        return jnp.where(lower, -rolled, rolled)

    def apply(table_idx, blocks):
        stacked = jnp.concatenate([
            jnp.concatenate(blocks, axis=1),
            jnp.concatenate([rot(b) for b in blocks], axis=1),
        ], axis=0)
        wide = jnp.dot(tab_ref[table_idx], stacked, preferred_element_type=jnp.float32)
        return [wide[:, g * lanes:(g + 1) * lanes] for g in range(len(blocks))]

    def scatter_y(a, middle):
        for hi in range(extent):
            y_ref[hi, a] = middle[hi * extent:(hi + 1) * extent]

    def stage_one(a0, blocks):
        for g, m in enumerate(apply(0, blocks)):
            scatter_y(a0 + g, m.astype(jnp.bfloat16))

    def write_out(a, value):
        for quarter in range(4):
            out_ref[(a % half_axis) * 4 + quarter, 0, a // half_axis] = value[quarter * rows:(quarter + 1) * rows]

    def init_group(i, carry):
        a0 = group * i
        initial = []
        for g in range(group):
            observed = obs(a0 + g)
            value = jnp.where(mask_ref[0, a0 + g] > 0, observed, jnp.zeros_like(observed))
            write_out(a0 + g, value)
            initial.append(value)
        stage_one(a0, initial)
        return carry

    lax.fori_loop(0, groups, init_group, 0, unroll=groups)

    def coeff_group(i):
        hi0 = group * i
        return apply(2, [y_ref[hi0 + g].reshape(plane, lanes) for g in range(group)])

    def init_hi(i, running):
        for coeffs in coeff_group(i):
            square = coeffs * coeffs
            running = jnp.maximum(running, jnp.max(square + pltpu.roll(square, half, 1), axis=0, keepdims=True))
        return running

    largest = jnp.sqrt(lax.fori_loop(0, groups, init_hi, jnp.zeros((1, lanes), jnp.float32), unroll=groups))

    def sweep_step(k, carry):
        cutoff = largest * scales_ref[k]

        def thin_group(i, c2):
            thinned = []
            blocks = coeff_group(i)
            for b in range(0, len(blocks), 2):
                first, second = blocks[b], blocks[b + 1]
                sq0 = first * first
                sq1 = second * second
                packed = jnp.where(lower, sq0 + pltpu.roll(sq0, half, 1), sq1 + pltpu.roll(sq1, half, 1))
                size_now = jnp.sqrt(packed)
                factor = jnp.maximum(size_now - cutoff, 0.0) / (jnp.maximum(size_now, cutoff) + 1e-06)
                swapped = pltpu.roll(factor, half, 1)
                thinned.append((first * jnp.where(lower, factor, swapped)).astype(jnp.bfloat16))
                thinned.append((second * jnp.where(lower, swapped, factor)).astype(jnp.bfloat16))
            hi0 = group * i
            for g, back_mid in enumerate(apply(3, thinned)):
                back_mid = back_mid.astype(jnp.bfloat16)
                for a in range(extent):
                    v_ref[a, hi0 + g] = back_mid[a * extent:(a + 1) * extent]
            return c2

        lax.fori_loop(0, groups, thin_group, 0, unroll=groups)

        def back_group(i, c2):
            a0 = group * i
            returned = apply(1, [v_ref[a0 + g].reshape(plane, lanes) for g in range(group)])
            updated = []
            for g in range(group):
                observed = obs(a0 + g).astype(jnp.float32)
                value = jnp.where(mask_ref[0, a0 + g] > 0, observed, returned[g]).astype(jnp.bfloat16)
                write_out(a0 + g, value)
                updated.append(value)

            @pl.when(k + 1 < sweeps)
            def _():
                stage_one(a0, updated)

            return c2

        lax.fori_loop(0, groups, back_group, 0, unroll=groups)
        return carry

    lax.fori_loop(0, sweeps, sweep_step, 0)


def run_patches(observed, maskb, sweeps, scales, tables):
    count, extent, plane, lanes = maskb.shape
    block = pl.BlockSpec((1, extent, plane, lanes), lambda p, c, s: (p, 0, 0, 0))
    sources = observed.shape[0]
    obs_block = pl.BlockSpec((sources, 1) + observed.shape[2:], lambda p, c, s: (0, p, 0, 0))
    dests = extent // 2 * 4
    out_block = pl.BlockSpec((dests, 1, 2, plane // 4, lanes), lambda p, c, s: (0, p, 0, 0, 0))
    grid_spec = pltpu.PrefetchScalarGridSpec(
        num_scalar_prefetch=2,
        grid=(count,),
        in_specs=[obs_block, block, pl.BlockSpec(tables.shape, lambda p, c, s: (0, 0, 0))],
        out_specs=out_block,
        scratch_shapes=[
            pltpu.VMEM((extent, extent, extent, lanes), jnp.bfloat16),
            pltpu.VMEM((extent, extent, extent, lanes), jnp.bfloat16),
        ],
    )
    return pl.pallas_call(
        pocs_kernel,
        grid_spec=grid_spec,
        out_shape=jax.ShapeDtypeStruct((dests, count, 2, plane // 4, lanes), jnp.bfloat16),
        compiler_params=pltpu.CompilerParams(dimension_semantics=("arbitrary",)),
    )(sweeps, scales, observed, maskb, tables)


def shards(spectra, sampled_mask, counts):
    extent = sampled_mask.shape[2]
    plane = extent * extent
    lane_count = spectra.shape[3]
    halfway = extent // 2
    devices = lax.axis_size("shot")
    owned_count = counts.shape[1]
    chunk = owned_count // 2
    tables = kernel_tables(extent)
    steps = jnp.arange(8, dtype=jnp.float32)
    scales = 0.5 * jnp.power(jnp.float32(0.6), steps)
    by_owner = spectra.reshape((1, devices, owned_count) + spectra.shape[2:])

    pieces = []
    for first in range(0, owned_count, chunk):
        part = by_owner[:, :, first:first + chunk]
        observed = lax.all_to_all(part, "shot", split_axis=1, concat_axis=1, tiled=True)[0]
        recorded = (sampled_mask[0, first:first + chunk] > 0).astype(jnp.bfloat16)
        maskb = jnp.broadcast_to(recorded[..., None], (chunk, extent, plane, lane_count))
        pieces.append(run_patches(observed, maskb, counts[0, first:first + chunk], scales, tables))
    result = jnp.concatenate(pieces, axis=1)
    dests = result.shape[0]
    top = result[:, :, 1]
    arrived = passed_along(top[:, -1], "shot", 1)
    earlier = jnp.concatenate([arrived[:, None], top[:, :-1]], axis=1).astype(jnp.float32)
    h = (jnp.arange(dests, dtype=jnp.int32) // (dests // halfway)).astype(jnp.float32)
    weight = ((h + 0.5) / halfway)[:, None, None, None]
    mixed = weight * result[:, :, 0].astype(jnp.float32) + (1.0 - weight) * earlier
    mixed = mixed.astype(jnp.bfloat16)
    return lax.all_to_all(mixed, "shot", split_axis=0, concat_axis=1, tiled=True)


def solution(mesh):
    return jax.shard_map(
        shards,
        mesh=mesh,
        in_specs=(P("az", None, "shot", None), P("az", "shot", None, None), P("az", "shot")),
        out_specs=P("az", None, "shot", None),
        check_vma=False,
    )
```
